32 devices in a mesh: ctx: 16 (over z, y, x), tp: 2 (over core).
Axes of the slice: x: 2, y: 2, z: 4, core: 2. Of those that a mesh axis runs over, the one named last changes fastest.
Arguments:
- x_act: bfloat16 [4096, 8192], P('ctx', 'tp'), may hold values from -0.119628906 to 0.119628906
- b_proj: bfloat16 [4096, 128], P('ctx'), may hold values from -0.5 to 0.5
- c_proj: bfloat16 [4096, 128], P('ctx'), may hold values from -0.5 to 0.5
- dt_raw: bfloat16 [4096, 128], P('ctx', 'tp'), may hold values from -3 to 3
- a_log: float32 [128], P('tp'), may hold values from -12 to -2
- d_skip: float32 [128], P('tp'), may hold values from 0.5 to 2
- grad_out: bfloat16 [4096, 8192], P('ctx', 'tp'), may hold values from -6 to 6
Outputs:
- grad_x: bfloat16 [4096, 8192], P('ctx', 'tp')
- grad_b: float32 [4096, 128], P('ctx')
- grad_c: float32 [4096, 128], P('ctx')
- grad_dt: bfloat16 [4096, 128], P('ctx', 'tp')
The draws below stay inside these ranges and needn't reach their ends.
All inputs are finite; a program needn't handle non-finite values.
Results may differ from the reference program's by a relative error of at most 0.001.
Values may be sent and summed in bfloat16 or wider, within the bound.
No kernel may reach another device: no remote copies, remote signals or barrier semaphores. Data moves between devices by JAX's collectives and lax.ppermute only.
A program may use at most 192 MiB of HBM per device.

```python
import jax
import jax.numpy as jnp
from jax import lax

HEADS = 128
HEAD_DIM = 64
STATE = 128
BLOCK = 256
SEQ = 4096


def draw_a_log(key, part):
    pick_key = jax.random.fold_in(key, 11)
    slow_key = jax.random.fold_in(key, 12)
    fast_key = jax.random.fold_in(key, 13)
    slow_share = 0.5
    choose = jax.random.uniform(pick_key, (HEADS,), jnp.float32) < slow_share
    slow_rate = 2.3 / (SEQ * 0.75) * jnp.exp(jax.random.uniform(slow_key, (HEADS,), jnp.float32, jnp.log(0.2), 0.0))
    fast_rate = jnp.exp(jax.random.uniform(fast_key, (HEADS,), jnp.float32, jnp.log(0.02), jnp.log(0.1)))
    return jnp.log(jnp.where(choose, slow_rate, fast_rate)).astype(jnp.float32)


def shard_levels(rng, shape, split, low, largest):
    factor_of = 1.0
    for dim, parts in split:
        heights = jax.random.uniform(jax.random.fold_in(jax.random.fold_in(rng, 6), dim), (parts,), jnp.float32, low / len(split), largest / len(split))
        factor_of = factor_of * jnp.repeat(jnp.exp(heights), shape[dim] // parts).reshape((-1,) + (1,) * (len(shape) - 1 - dim))
    return factor_of


def gaussian(own_key, dims, deviation, bound, cuts=(), kind=jnp.bfloat16):
    values = jax.random.normal(own_key, dims, jnp.float32) * deviation
    if len(cuts) > 0:
        values = shard_levels(own_key, dims, cuts, -0.22, 0.18) * values
    return jnp.clip(values, min=-bound, max=bound).astype(kind)


def setup_inputs(seed: int = 0) -> dict:
    streams_of = jax.random.split(jax.random.key(seed), 8)
    x_act = gaussian(streams_of[0], (SEQ, HEADS * HEAD_DIM), 0.02, 0.119628906, ((0, 16), (1, 2)))
    b_proj = gaussian(streams_of[1], (SEQ, STATE), STATE ** -0.5, 0.5, ((0, 16),))
    c_proj = gaussian(streams_of[2], (SEQ, STATE), STATE ** -0.5, 0.5, ((0, 16),))
    dt_raw = gaussian(streams_of[3], (SEQ, HEADS), 0.5, 3.0, ((0, 16), (1, 2)))
    a_log = draw_a_log(jax.random.fold_in(streams_of[7], 71), 0)
    d_skip = jnp.clip(0.5 + 1.5 * jax.random.uniform(streams_of[5], (HEADS,), jnp.float32) ** shard_levels(streams_of[5], (HEADS,), ((0, 2),), -0.2, 0.2), 0.5, 2.0)
    grad_out = gaussian(streams_of[6], (SEQ, HEADS * HEAD_DIM), 1.0, 6.0, ((0, 16), (1, 2)))
    return dict(x_act=x_act, b_proj=b_proj, c_proj=c_proj, dt_raw=dt_raw, a_log=a_log, d_skip=d_skip, grad_out=grad_out)


precise = lax.Precision.HIGHEST

def head_forward(x_head, b_rows, c_rows, raw_step, log_rate, skip_gain, start_state, block_len):
    length, head_width = x_head.shape
    blocks = length // block_len
    step_size = jax.nn.softplus(raw_step)
    decay_rates = -jnp.exp(log_rate) * step_size
    row_index = lax.broadcasted_iota(jnp.int32, (block_len, block_len), 0)
    col_index = lax.broadcasted_iota(jnp.int32, (block_len, block_len), 1)
    lower_mask = row_index >= col_index
    running = jnp.dot(decay_rates.reshape(blocks, block_len), lower_mask.astype(jnp.float32).T, precision=precise)
    between = jnp.where(lower_mask[None], running[:, :, None] - running[:, None, :], -1e+30)
    x_blocks = x_head.reshape(blocks, block_len, head_width)
    b_blocks = b_rows.reshape(blocks, block_len, -1)
    c_blocks = c_rows.reshape(blocks, block_len, -1)
    s_blocks = step_size.reshape(blocks, block_len)
    scores = jnp.einsum('kin,kjn->kij', c_blocks, b_blocks, precision=precise) * jnp.exp(between) * s_blocks[:, None, :]
    output = jnp.einsum('kij,kjp->kip', scores, x_blocks, precision=precise)
    closing = running[:, -1]
    weighted = (jnp.exp(closing[:, None] - running) * s_blocks)[:, :, None] * x_blocks
    states = jnp.einsum('kjp,kjn->kpn', weighted, b_blocks, precision=precise)
    block_rows = lax.broadcasted_iota(jnp.int32, (blocks, blocks), 0)
    block_cols = lax.broadcasted_iota(jnp.int32, (blocks, blocks), 1)
    through = jnp.dot((block_rows >= block_cols).astype(jnp.float32), closing, precision=precise)
    before = through - closing
    carry_weight = jnp.exp(jnp.where(block_rows > block_cols, before[:, None] - through[None, :], -1e+30))
    entering = jnp.einsum('kj,jpn->kpn', carry_weight, states, precision=precise) + jnp.exp(before)[:, None, None] * start_state[None]
    reading = jnp.exp(running)[:, :, None] * c_blocks
    output = output + jnp.einsum('kin,kpn->kip', reading, entering, precision=precise)
    output = output.reshape(length, head_width) + skip_gain * x_head
    final_state = jnp.einsum('j,jpn->pn', jnp.exp(through[-1] - through), states, precision=precise) + jnp.exp(through[-1]) * start_state
    return (output, final_state)

def reference(x_act, b_proj, c_proj, dt_raw, a_log, d_skip, grad_out):
    b_rows = b_proj.astype(jnp.float32)
    c_rows = c_proj.astype(jnp.float32)
    x_heads = x_act.reshape(SEQ, HEADS, HEAD_DIM).transpose(1, 0, 2)
    g_heads = grad_out.reshape(SEQ, HEADS, HEAD_DIM).transpose(1, 0, 2)
    raw_heads = dt_raw.astype(jnp.float32).T
    anchor_state = jnp.zeros((HEAD_DIM, STATE), jnp.float32)

    def per_head(totals, head_item):
        x_one, g_one, raw_one, rate_one, gain_one = head_item

        def forward(x_val, b_val, c_val, raw_val):
            return head_forward(x_val, b_val, c_val, raw_val, rate_one, gain_one, anchor_state, BLOCK)[0]
        outcome, pullback = jax.vjp(forward, x_one.astype(jnp.float32), b_rows, c_rows, raw_one)
        grad_xh, grad_bh, grad_ch, grad_raw = pullback(g_one.astype(jnp.float32))
        return ((totals[0] + grad_bh, totals[1] + grad_ch), (grad_xh.astype(jnp.bfloat16), grad_raw.astype(jnp.bfloat16)))
    blank_rows = jnp.zeros((SEQ, STATE), jnp.float32)
    totals_out, stacked = lax.scan(per_head, (blank_rows, blank_rows), (x_heads, g_heads, raw_heads, a_log, d_skip))
    grad_x = stacked[0].transpose(1, 0, 2).reshape(SEQ, HEADS * HEAD_DIM)
    grad_dt = stacked[1].T
    return (grad_x, totals_out[0], totals_out[1], grad_dt)
```

```python
from functools import partial

import jax
import jax.numpy as jnp
from jax import lax
from jax.sharding import PartitionSpec as P

BLOCK = 256


precise = lax.Precision.HIGHEST


def head_forward(x_head, b_rows, c_rows, raw_step, log_rate, skip_gain, start_state, block_len):
    length, head_width = x_head.shape
    blocks = length // block_len
    step_size = jax.nn.softplus(raw_step)
    decay_rates = -jnp.exp(log_rate) * step_size
    row_index = lax.broadcasted_iota(jnp.int32, (block_len, block_len), 0)
    col_index = lax.broadcasted_iota(jnp.int32, (block_len, block_len), 1)
    lower_mask = row_index >= col_index
    running = jnp.dot(
        decay_rates.reshape(blocks, block_len), lower_mask.astype(jnp.float32).T, precision=precise
    )
    between = jnp.where(lower_mask[None], running[:, :, None] - running[:, None, :], -1e30)
    x_blocks = x_head.reshape(blocks, block_len, head_width)
    b_blocks = b_rows.reshape(blocks, block_len, -1)
    c_blocks = c_rows.reshape(blocks, block_len, -1)
    s_blocks = step_size.reshape(blocks, block_len)
    scores = (
        jnp.einsum("kin,kjn->kij", c_blocks, b_blocks, precision=precise)
        * jnp.exp(between)
        * s_blocks[:, None, :]
    )
    output = jnp.einsum("kij,kjp->kip", scores, x_blocks, precision=precise)
    closing = running[:, -1]
    weighted = (jnp.exp(closing[:, None] - running) * s_blocks)[:, :, None] * x_blocks
    states = jnp.einsum("kjp,kjn->kpn", weighted, b_blocks, precision=precise)
    block_rows = lax.broadcasted_iota(jnp.int32, (blocks, blocks), 0)
    block_cols = lax.broadcasted_iota(jnp.int32, (blocks, blocks), 1)
    through = jnp.dot((block_rows >= block_cols).astype(jnp.float32), closing, precision=precise)
    before = through - closing
    carry_weight = jnp.exp(
        jnp.where(block_rows > block_cols, before[:, None] - through[None, :], -1e30)
    )
    entering = (
        jnp.einsum("kj,jpn->kpn", carry_weight, states, precision=precise)
        + jnp.exp(before)[:, None, None] * start_state[None]
    )
    reading = jnp.exp(running)[:, :, None] * c_blocks
    output = output + jnp.einsum("kin,kpn->kip", reading, entering, precision=precise)
    output = output.reshape(length, head_width) + skip_gain * x_head
    final_state = (
        jnp.einsum("j,jpn->pn", jnp.exp(through[-1] - through), states, precision=precise)
        + jnp.exp(through[-1]) * start_state
    )
    return (output, final_state)


N_CHUNKS = 1


def chunk_backward(x_seq, g_seq, raw_seq, b_rows, c_rows, rate, gain):
    length = x_seq.shape[0]
    heads = raw_seq.shape[1]
    head_width = x_seq.shape[1] // heads
    runner = partial(head_forward, block_len=BLOCK)
    mapped = jax.vmap(runner, in_axes=(0, None, None, 0, 0, 0, 0))
    x_heads = x_seq.astype(jnp.float32).reshape(length, heads, head_width).transpose(1, 0, 2)
    g_heads = g_seq.astype(jnp.float32).reshape(length, heads, head_width).transpose(1, 0, 2)
    raw_heads = raw_seq.astype(jnp.float32).T
    anchor = jnp.zeros((heads, head_width, b_rows.shape[1]), jnp.float32)

    def forward(x_val, b_val, c_val, raw_val):
        return mapped(x_val, b_val, c_val, raw_val, rate, gain, anchor)[0]

    _, pullback = jax.vjp(forward, x_heads, b_rows, c_rows, raw_heads)
    grad_xh, grad_b_all, grad_c_all, grad_raw = pullback(g_heads)
    x_back = grad_xh.transpose(1, 0, 2).reshape(length, heads * head_width).astype(jnp.bfloat16)
    raw_back = grad_raw.T.astype(jnp.bfloat16)
    return x_back, raw_back, grad_b_all, grad_c_all


def local(x_act, b_proj, c_proj, dt_raw, a_log, d_skip, grad_out):
    rows = x_act.shape[0]
    heads_here = dt_raw.shape[1]
    head_width = x_act.shape[1] // heads_here
    state = b_proj.shape[1]
    owners = lax.axis_size("ctx")
    per_owner = heads_here // owners
    chunks = N_CHUNKS if per_owner % N_CHUNKS == 0 else 1
    per_chunk = per_owner // chunks
    me = lax.axis_index("ctx")
    half = lax.axis_index("tp")

    bc_seq = lax.all_gather(jnp.concatenate([b_proj, c_proj], axis=1), "ctx", axis=0, tiled=True)
    b_rows = bc_seq[:, :state].astype(jnp.float32)
    c_rows = bc_seq[:, state:].astype(jnp.float32)
    first_head = me * per_owner
    rate_own = lax.dynamic_slice_in_dim(a_log, first_head, per_owner)
    gain_own = lax.dynamic_slice_in_dim(d_skip, first_head, per_owner)

    x4 = x_act.reshape(rows, owners, per_owner, head_width)
    g4 = grad_out.reshape(rows, owners, per_owner, head_width)
    r3 = dt_raw.reshape(rows, owners, per_owner)
    x_parts, raw_parts = [], []
    grad_b_all = None
    grad_c_all = None
    for c in range(chunks):
        sl = slice(c * per_chunk, (c + 1) * per_chunk)
        width = per_chunk * head_width
        xg = jnp.concatenate(
            [x4[:, :, sl, :].reshape(rows, owners, width), g4[:, :, sl, :].reshape(rows, owners, width)], axis=2
        )
        xg_seq = lax.all_to_all(xg, "ctx", split_axis=1, concat_axis=0, tiled=True).reshape(rows * owners, 2 * width)
        raw_seq = lax.all_to_all(r3[:, :, sl], "ctx", split_axis=1, concat_axis=0, tiled=True).reshape(
            rows * owners, per_chunk
        )
        x_back, raw_back, gb, gc = chunk_backward(
            xg_seq[:, :width], xg_seq[:, width:], raw_seq, b_rows, c_rows, rate_own[sl], gain_own[sl]
        )
        x_parts.append(
            lax.all_to_all(x_back, "ctx", split_axis=0, concat_axis=1, tiled=True).reshape(rows, owners, 1, width)
        )
        raw_parts.append(
            lax.all_to_all(raw_back, "ctx", split_axis=0, concat_axis=1, tiled=True).reshape(rows, owners, 1, per_chunk)
        )
        grad_b_all = gb if grad_b_all is None else grad_b_all + gb
        grad_c_all = gc if grad_c_all is None else grad_c_all + gc
    grad_x = jnp.concatenate(x_parts, axis=2).reshape(rows, owners * per_owner * head_width)
    grad_dt = jnp.concatenate(raw_parts, axis=2).reshape(rows, heads_here)

    is_first = half == 0
    send = jnp.where(is_first, grad_c_all, grad_b_all)
    keep = jnp.where(is_first, grad_b_all, grad_c_all)
    mine = keep + lax.ppermute(send, "tp", [(0, 1), (1, 0)])
    parts = lax.all_to_all(mine.reshape(owners, rows, state), "ctx", split_axis=0, concat_axis=0, tiled=True)
    mine = parts.sum(axis=0)
    other = lax.ppermute(mine, "tp", [(0, 1), (1, 0)])
    grad_b = jnp.where(is_first, mine, other)
    grad_c = jnp.where(is_first, other, mine)
    return (grad_x, grad_b, grad_c, grad_dt)


def solution(mesh):
    in_specs = (
        P("ctx", "tp"),
        P("ctx", None),
        P("ctx", None),
        P("ctx", "tp"),
        P("tp"),
        P("tp"),
        P("ctx", "tp"),
    )
    out_specs = (P("ctx", "tp"), P("ctx", None), P("ctx", None), P("ctx", "tp"))
    return jax.shard_map(local, mesh=mesh, in_specs=in_specs, out_specs=out_specs, check_vma=False)
```

```python
from functools import partial

import jax
import jax.numpy as jnp
from jax import lax
from jax.sharding import PartitionSpec as P

BLOCK = 256


precise = lax.Precision.HIGHEST


def head_forward(x_head, b_rows, c_rows, raw_step, log_rate, skip_gain, start_state, block_len):
    length, head_width = x_head.shape
    blocks = length // block_len
    step_size = jax.nn.softplus(raw_step)
    decay_rates = -jnp.exp(log_rate) * step_size
    row_index = lax.broadcasted_iota(jnp.int32, (block_len, block_len), 0)
    col_index = lax.broadcasted_iota(jnp.int32, (block_len, block_len), 1)
    lower_mask = row_index >= col_index
    running = jnp.dot(
        decay_rates.reshape(blocks, block_len), lower_mask.astype(jnp.float32).T, precision=precise
    )
    between = jnp.where(lower_mask[None], running[:, :, None] - running[:, None, :], -1e30)
    x_blocks = x_head.reshape(blocks, block_len, head_width)
    b_blocks = b_rows.reshape(blocks, block_len, -1)
    c_blocks = c_rows.reshape(blocks, block_len, -1)
    s_blocks = step_size.reshape(blocks, block_len)
    scores = (
        jnp.einsum("kin,kjn->kij", c_blocks, b_blocks, precision=precise)
        * jnp.exp(between)
        * s_blocks[:, None, :]
    )
    output = jnp.einsum("kij,kjp->kip", scores, x_blocks, precision=precise)
    closing = running[:, -1]
    weighted = (jnp.exp(closing[:, None] - running) * s_blocks)[:, :, None] * x_blocks
    states = jnp.einsum("kjp,kjn->kpn", weighted, b_blocks, precision=precise)
    block_rows = lax.broadcasted_iota(jnp.int32, (blocks, blocks), 0)
    block_cols = lax.broadcasted_iota(jnp.int32, (blocks, blocks), 1)
    through = jnp.dot((block_rows >= block_cols).astype(jnp.float32), closing, precision=precise)
    before = through - closing
    carry_weight = jnp.exp(
        jnp.where(block_rows > block_cols, before[:, None] - through[None, :], -1e30)
    )
    entering = (
        jnp.einsum("kj,jpn->kpn", carry_weight, states, precision=precise)
        + jnp.exp(before)[:, None, None] * start_state[None]
    )
    reading = jnp.exp(running)[:, :, None] * c_blocks
    output = output + jnp.einsum("kin,kpn->kip", reading, entering, precision=precise)
    output = output.reshape(length, head_width) + skip_gain * x_head
    final_state = (
        jnp.einsum("j,jpn->pn", jnp.exp(through[-1] - through), states, precision=precise)
        + jnp.exp(through[-1]) * start_state
    )
    return (output, final_state)


N_CHUNKS = 2


def chunk_backward(x_seq, g_seq, raw_seq, b_rows, c_rows, rate, gain):
    length = x_seq.shape[0]
    heads = raw_seq.shape[1]
    head_width = x_seq.shape[1] // heads
    runner = partial(head_forward, block_len=BLOCK)
    mapped = jax.vmap(runner, in_axes=(0, None, None, 0, 0, 0, 0))
    x_heads = x_seq.astype(jnp.float32).reshape(length, heads, head_width).transpose(1, 0, 2)
    g_heads = g_seq.astype(jnp.float32).reshape(length, heads, head_width).transpose(1, 0, 2)
    raw_heads = raw_seq.astype(jnp.float32).T
    anchor = jnp.zeros((heads, head_width, b_rows.shape[1]), jnp.float32)

    def forward(x_val, b_val, c_val, raw_val):
        return mapped(x_val, b_val, c_val, raw_val, rate, gain, anchor)[0]

    _, pullback = jax.vjp(forward, x_heads, b_rows, c_rows, raw_heads)
    grad_xh, grad_b_all, grad_c_all, grad_raw = pullback(g_heads)
    x_back = grad_xh.transpose(1, 0, 2).reshape(length, heads * head_width).astype(jnp.bfloat16)
    raw_back = grad_raw.T.astype(jnp.bfloat16)
    return x_back, raw_back, grad_b_all, grad_c_all


def local(x_act, b_proj, c_proj, dt_raw, a_log, d_skip, grad_out):
    rows = x_act.shape[0]
    heads_here = dt_raw.shape[1]
    head_width = x_act.shape[1] // heads_here
    state = b_proj.shape[1]
    owners = lax.axis_size("ctx")
    per_owner = heads_here // owners
    chunks = N_CHUNKS if per_owner % N_CHUNKS == 0 else 1
    per_chunk = per_owner // chunks
    me = lax.axis_index("ctx")
    half = lax.axis_index("tp")

    first_head = me * per_owner
    rate_own = lax.dynamic_slice_in_dim(a_log, first_head, per_owner)
    gain_own = lax.dynamic_slice_in_dim(d_skip, first_head, per_owner)

    x4 = x_act.reshape(rows, owners, per_owner, head_width)
    g4 = grad_out.reshape(rows, owners, per_owner, head_width)
    r3 = dt_raw.reshape(rows, owners, per_owner)
    x_parts, raw_parts = [], []
    grad_b_all = None
    grad_c_all = None
    for c in range(chunks):
        sl = slice(c * per_chunk, (c + 1) * per_chunk)
        width = per_chunk * head_width
        pieces = [x4[:, :, sl, :].reshape(rows, owners, width), g4[:, :, sl, :].reshape(rows, owners, width)]
        if c == 0:
            own_proj = jnp.where(half == 0, b_proj, c_proj)
            pieces.append(jnp.broadcast_to(own_proj[:, None, :], (rows, owners, state)))
        xg = jnp.concatenate(pieces, axis=2)
        xg_seq = lax.all_to_all(xg, "ctx", split_axis=1, concat_axis=0, tiled=True).reshape(rows * owners, -1)
        if c == 0:
            own_seq = xg_seq[:, 2 * width :]
            other_seq = lax.ppermute(own_seq, "tp", [(0, 1), (1, 0)])
            b_rows = jnp.where(half == 0, own_seq, other_seq).astype(jnp.float32)
            c_rows = jnp.where(half == 0, other_seq, own_seq).astype(jnp.float32)
        raw_seq = lax.all_to_all(r3[:, :, sl], "ctx", split_axis=1, concat_axis=0, tiled=True).reshape(
            rows * owners, per_chunk
        )
        x_back, raw_back, gb, gc = chunk_backward(
            xg_seq[:, :width], xg_seq[:, width : 2 * width], raw_seq, b_rows, c_rows, rate_own[sl], gain_own[sl]
        )
        x_parts.append(
            lax.all_to_all(x_back, "ctx", split_axis=0, concat_axis=1, tiled=True).reshape(rows, owners, 1, width)
        )
        raw_parts.append(
            lax.all_to_all(raw_back, "ctx", split_axis=0, concat_axis=1, tiled=True).reshape(rows, owners, 1, per_chunk)
        )
        grad_b_all = gb if grad_b_all is None else grad_b_all + gb
        grad_c_all = gc if grad_c_all is None else grad_c_all + gc
    grad_x = jnp.concatenate(x_parts, axis=2).reshape(rows, owners * per_owner * head_width)
    grad_dt = jnp.concatenate(raw_parts, axis=2).reshape(rows, heads_here)

    is_first = half == 0
    send = jnp.where(is_first, grad_c_all, grad_b_all)
    keep = jnp.where(is_first, grad_b_all, grad_c_all)
    mine = keep + lax.ppermute(send, "tp", [(0, 1), (1, 0)])
    parts = lax.all_to_all(mine.reshape(owners, rows, state), "ctx", split_axis=0, concat_axis=0, tiled=True)
    mine = parts.sum(axis=0)
    other = lax.ppermute(mine, "tp", [(0, 1), (1, 0)])
    grad_b = jnp.where(is_first, mine, other)
    grad_c = jnp.where(is_first, other, mine)
    return (grad_x, grad_b, grad_c, grad_dt)


def solution(mesh):
    in_specs = (
        P("ctx", "tp"),
        P("ctx", None),
        P("ctx", None),
        P("ctx", "tp"),
        P("tp"),
        P("tp"),
        P("ctx", "tp"),
    )
    out_specs = (P("ctx", "tp"), P("ctx", None), P("ctx", None), P("ctx", "tp"))
    return jax.shard_map(local, mesh=mesh, in_specs=in_specs, out_specs=out_specs, check_vma=False)
```

```python
from functools import partial

import jax
import jax.numpy as jnp
from jax import lax
from jax.sharding import PartitionSpec as P

BLOCK = 256


precise = lax.Precision.HIGHEST


def head_forward(x_head, b_rows, c_rows, raw_step, log_rate, skip_gain, start_state, block_len):
    length, head_width = x_head.shape
    blocks = length // block_len
    step_size = jax.nn.softplus(raw_step)
    decay_rates = -jnp.exp(log_rate) * step_size
    row_index = lax.broadcasted_iota(jnp.int32, (block_len, block_len), 0)
    col_index = lax.broadcasted_iota(jnp.int32, (block_len, block_len), 1)
    lower_mask = row_index >= col_index
    running = jnp.dot(
        decay_rates.reshape(blocks, block_len), lower_mask.astype(jnp.float32).T, precision=precise
    )
    between = jnp.where(lower_mask[None], running[:, :, None] - running[:, None, :], -1e30)
    x_blocks = x_head.reshape(blocks, block_len, head_width)
    b_blocks = b_rows.reshape(blocks, block_len, -1)
    c_blocks = c_rows.reshape(blocks, block_len, -1)
    s_blocks = step_size.reshape(blocks, block_len)
    scores = (
        jnp.einsum("kin,kjn->kij", c_blocks, b_blocks, precision=precise)
        * jnp.exp(between)
        * s_blocks[:, None, :]
    )
    output = jnp.einsum("kij,kjp->kip", scores, x_blocks, precision=precise)
    closing = running[:, -1]
    weighted = (jnp.exp(closing[:, None] - running) * s_blocks)[:, :, None] * x_blocks
    states = jnp.einsum("kjp,kjn->kpn", weighted, b_blocks, precision=precise)
    block_rows = lax.broadcasted_iota(jnp.int32, (blocks, blocks), 0)
    block_cols = lax.broadcasted_iota(jnp.int32, (blocks, blocks), 1)
    through = jnp.dot((block_rows >= block_cols).astype(jnp.float32), closing, precision=precise)
    before = through - closing
    carry_weight = jnp.exp(
        jnp.where(block_rows > block_cols, before[:, None] - through[None, :], -1e30)
    )
    entering = (
        jnp.einsum("kj,jpn->kpn", carry_weight, states, precision=precise)
        + jnp.exp(before)[:, None, None] * start_state[None]
    )
    reading = jnp.exp(running)[:, :, None] * c_blocks
    output = output + jnp.einsum("kin,kpn->kip", reading, entering, precision=precise)
    output = output.reshape(length, head_width) + skip_gain * x_head
    final_state = (
        jnp.einsum("j,jpn->pn", jnp.exp(through[-1] - through), states, precision=precise)
        + jnp.exp(through[-1]) * start_state
    )
    return (output, final_state)


N_CHUNKS = 1


def chunk_backward(x_seq, g_seq, raw_seq, b_rows, c_rows, rate, gain):
    length = x_seq.shape[0]
    heads = raw_seq.shape[1]
    head_width = x_seq.shape[1] // heads
    runner = partial(head_forward, block_len=BLOCK)
    mapped = jax.vmap(runner, in_axes=(0, None, None, 0, 0, 0, 0))
    x_heads = x_seq.astype(jnp.float32).reshape(length, heads, head_width).transpose(1, 0, 2)
    g_heads = g_seq.astype(jnp.float32).reshape(length, heads, head_width).transpose(1, 0, 2)
    raw_heads = raw_seq.astype(jnp.float32).T
    anchor = jnp.zeros((heads, head_width, b_rows.shape[1]), jnp.float32)

    def forward(x_val, b_val, c_val, raw_val):
        return mapped(x_val, b_val, c_val, raw_val, rate, gain, anchor)[0]

    _, pullback = jax.vjp(forward, x_heads, b_rows, c_rows, raw_heads)
    grad_xh, grad_b_all, grad_c_all, grad_raw = pullback(g_heads)
    x_back = grad_xh.transpose(1, 0, 2).reshape(length, heads * head_width).astype(jnp.bfloat16)
    raw_back = grad_raw.T.astype(jnp.bfloat16)
    return x_back, raw_back, grad_b_all, grad_c_all


def local(x_act, b_proj, c_proj, dt_raw, a_log, d_skip, grad_out):
    rows = x_act.shape[0]
    heads_here = dt_raw.shape[1]
    head_width = x_act.shape[1] // heads_here
    state = b_proj.shape[1]
    owners = lax.axis_size("ctx")
    per_owner = heads_here // owners
    chunks = N_CHUNKS if per_owner % N_CHUNKS == 0 else 1
    per_chunk = per_owner // chunks
    me = lax.axis_index("ctx")
    half = lax.axis_index("tp")

    first_head = me * per_owner
    rate_own = lax.dynamic_slice_in_dim(a_log, first_head, per_owner)
    gain_own = lax.dynamic_slice_in_dim(d_skip, first_head, per_owner)

    x4 = x_act.reshape(rows, owners, per_owner, head_width)
    g4 = grad_out.reshape(rows, owners, per_owner, head_width)
    r3 = dt_raw.reshape(rows, owners, per_owner)
    x_parts, raw_parts = [], []
    grad_b_all = None
    grad_c_all = None
    for c in range(chunks):
        sl = slice(c * per_chunk, (c + 1) * per_chunk)
        width = per_chunk * head_width
        pieces = [x4[:, :, sl, :].reshape(rows, owners, width), g4[:, :, sl, :].reshape(rows, owners, width)]
        if c == 0:
            own_proj = jnp.where(half == 0, b_proj, c_proj)
            pieces.append(jnp.broadcast_to(own_proj[:, None, :], (rows, owners, state)))
        xg = jnp.concatenate(pieces, axis=2)
        xg_seq = lax.all_to_all(xg, "ctx", split_axis=1, concat_axis=0, tiled=True).reshape(rows * owners, -1)
        if c == 0:
            own_seq = xg_seq[:, 2 * width :]
            other_seq = lax.ppermute(own_seq, "tp", [(0, 1), (1, 0)])
            b_rows = jnp.where(half == 0, own_seq, other_seq).astype(jnp.float32)
            c_rows = jnp.where(half == 0, other_seq, own_seq).astype(jnp.float32)
        raw_seq = lax.all_to_all(r3[:, :, sl], "ctx", split_axis=1, concat_axis=0, tiled=True).reshape(
            rows * owners, per_chunk
        )
        x_back, raw_back, gb, gc = chunk_backward(
            xg_seq[:, :width], xg_seq[:, width : 2 * width], raw_seq, b_rows, c_rows, rate_own[sl], gain_own[sl]
        )
        x_parts.append(
            lax.all_to_all(x_back, "ctx", split_axis=0, concat_axis=1, tiled=True).reshape(rows, owners, 1, width)
        )
        raw_parts.append(
            lax.all_to_all(raw_back, "ctx", split_axis=0, concat_axis=1, tiled=True).reshape(rows, owners, 1, per_chunk)
        )
        grad_b_all = gb if grad_b_all is None else grad_b_all + gb
        grad_c_all = gc if grad_c_all is None else grad_c_all + gc
    grad_x = jnp.concatenate(x_parts, axis=2).reshape(rows, owners * per_owner * head_width)
    grad_dt = jnp.concatenate(raw_parts, axis=2).reshape(rows, heads_here)

    is_first = half == 0
    send = jnp.where(is_first, grad_c_all, grad_b_all)
    keep = jnp.where(is_first, grad_b_all, grad_c_all)
    mine = keep + lax.ppermute(send, "tp", [(0, 1), (1, 0)])
    parts = lax.all_to_all(mine.reshape(owners, rows, state), "ctx", split_axis=0, concat_axis=0, tiled=True)
    mine = parts.sum(axis=0)
    other = lax.ppermute(mine, "tp", [(0, 1), (1, 0)])
    grad_b = jnp.where(is_first, mine, other)
    grad_c = jnp.where(is_first, other, mine)
    return (grad_x, grad_b, grad_c, grad_dt)


def solution(mesh):
    in_specs = (
        P("ctx", "tp"),
        P("ctx", None),
        P("ctx", None),
        P("ctx", "tp"),
        P("tp"),
        P("tp"),
        P("ctx", "tp"),
    )
    out_specs = (P("ctx", "tp"), P("ctx", None), P("ctx", None), P("ctx", "tp"))
    return jax.shard_map(local, mesh=mesh, in_specs=in_specs, out_specs=out_specs, check_vma=False)
```

```python
from functools import partial

import jax
import jax.numpy as jnp
from jax import lax
from jax.sharding import PartitionSpec as P

BLOCK = 256


precise = lax.Precision.HIGHEST


def head_forward(x_head, b_rows, c_rows, raw_step, log_rate, skip_gain, start_state, block_len):
    length, head_width = x_head.shape
    blocks = length // block_len
    step_size = jax.nn.softplus(raw_step)
    decay_rates = -jnp.exp(log_rate) * step_size
    row_index = lax.broadcasted_iota(jnp.int32, (block_len, block_len), 0)
    col_index = lax.broadcasted_iota(jnp.int32, (block_len, block_len), 1)
    lower_mask = row_index >= col_index
    running = jnp.dot(
        decay_rates.reshape(blocks, block_len), lower_mask.astype(jnp.float32).T, precision=precise
    )
    between = jnp.where(lower_mask[None], running[:, :, None] - running[:, None, :], -1e30)
    x_blocks = x_head.reshape(blocks, block_len, head_width)
    b_blocks = b_rows.reshape(blocks, block_len, -1)
    c_blocks = c_rows.reshape(blocks, block_len, -1)
    s_blocks = step_size.reshape(blocks, block_len)
    scores = (
        jnp.einsum("kin,kjn->kij", c_blocks, b_blocks, precision=precise)
        * jnp.exp(between)
        * s_blocks[:, None, :]
    )
    output = jnp.einsum("kij,kjp->kip", scores, x_blocks, precision=precise)
    closing = running[:, -1]
    weighted = (jnp.exp(closing[:, None] - running) * s_blocks)[:, :, None] * x_blocks
    states = jnp.einsum("kjp,kjn->kpn", weighted, b_blocks, precision=precise)
    block_rows = lax.broadcasted_iota(jnp.int32, (blocks, blocks), 0)
    block_cols = lax.broadcasted_iota(jnp.int32, (blocks, blocks), 1)
    through = jnp.dot((block_rows >= block_cols).astype(jnp.float32), closing, precision=precise)
    before = through - closing
    carry_weight = jnp.exp(
        jnp.where(block_rows > block_cols, before[:, None] - through[None, :], -1e30)
    )
    entering = (
        jnp.einsum("kj,jpn->kpn", carry_weight, states, precision=precise)
        + jnp.exp(before)[:, None, None] * start_state[None]
    )
    reading = jnp.exp(running)[:, :, None] * c_blocks
    output = output + jnp.einsum("kin,kpn->kip", reading, entering, precision=precise)
    output = output.reshape(length, head_width) + skip_gain * x_head
    final_state = (
        jnp.einsum("j,jpn->pn", jnp.exp(through[-1] - through), states, precision=precise)
        + jnp.exp(through[-1]) * start_state
    )
    return (output, final_state)


N_CHUNKS = 1


def chunk_backward(x_seq, g_seq, raw_seq, b_rows, c_rows, rate, gain):
    length = x_seq.shape[0]
    heads = raw_seq.shape[1]
    head_width = x_seq.shape[1] // heads
    runner = partial(head_forward, block_len=BLOCK)
    mapped = jax.vmap(runner, in_axes=(0, None, None, 0, 0, 0, 0))
    x_heads = x_seq.astype(jnp.float32).reshape(length, heads, head_width).transpose(1, 0, 2)
    g_heads = g_seq.astype(jnp.float32).reshape(length, heads, head_width).transpose(1, 0, 2)
    raw_heads = raw_seq.astype(jnp.float32).T
    anchor = jnp.zeros((heads, head_width, b_rows.shape[1]), jnp.float32)

    def forward(x_val, b_val, c_val, raw_val):
        return mapped(x_val, b_val, c_val, raw_val, rate, gain, anchor)[0]

    _, pullback = jax.vjp(forward, x_heads, b_rows, c_rows, raw_heads)
    grad_xh, grad_b_all, grad_c_all, grad_raw = pullback(g_heads)
    x_back = grad_xh.transpose(1, 0, 2).reshape(length, heads * head_width).astype(jnp.bfloat16)
    raw_back = grad_raw.T.astype(jnp.bfloat16)
    return x_back, raw_back, grad_b_all, grad_c_all


def gather_ctx(block, owners, me):
    if owners & (owners - 1):
        return lax.all_gather(block, "ctx", axis=0, tiled=True)
    have = block
    step = 1
    while step < owners:
        theirs = lax.ppermute(have, "ctx", [(k, k ^ step) for k in range(owners)])
        upper = (me // step) % 2 == 1
        have = jnp.where(upper, jnp.concatenate([theirs, have]), jnp.concatenate([have, theirs]))
        step *= 2
    return have


def local(x_act, b_proj, c_proj, dt_raw, a_log, d_skip, grad_out):
    rows = x_act.shape[0]
    heads_here = dt_raw.shape[1]
    head_width = x_act.shape[1] // heads_here
    state = b_proj.shape[1]
    owners = lax.axis_size("ctx")
    per_owner = heads_here // owners
    chunks = N_CHUNKS if per_owner % N_CHUNKS == 0 else 1
    per_chunk = per_owner // chunks
    me = lax.axis_index("ctx")
    half = lax.axis_index("tp")

    own_seq = gather_ctx(jnp.where(half == 0, b_proj, c_proj), owners, me)
    other_seq = lax.ppermute(own_seq, "tp", [(0, 1), (1, 0)])
    b_rows = jnp.where(half == 0, own_seq, other_seq).astype(jnp.float32)
    c_rows = jnp.where(half == 0, other_seq, own_seq).astype(jnp.float32)
    first_head = me * per_owner
    rate_own = lax.dynamic_slice_in_dim(a_log, first_head, per_owner)
    gain_own = lax.dynamic_slice_in_dim(d_skip, first_head, per_owner)

    x4 = x_act.reshape(rows, owners, per_owner, head_width)
    g4 = grad_out.reshape(rows, owners, per_owner, head_width)
    r3 = dt_raw.reshape(rows, owners, per_owner)
    x_parts, raw_parts = [], []
    grad_b_all = None
    grad_c_all = None
    for c in range(chunks):
        sl = slice(c * per_chunk, (c + 1) * per_chunk)
        width = per_chunk * head_width
        pieces = [x4[:, :, sl, :].reshape(rows, owners, width), g4[:, :, sl, :].reshape(rows, owners, width)]
        xg = jnp.concatenate(pieces, axis=2)
        xg_seq = lax.all_to_all(xg, "ctx", split_axis=1, concat_axis=0, tiled=True).reshape(rows * owners, -1)
        raw_seq = lax.all_to_all(r3[:, :, sl], "ctx", split_axis=1, concat_axis=0, tiled=True).reshape(
            rows * owners, per_chunk
        )
        x_back, raw_back, gb, gc = chunk_backward(
            xg_seq[:, :width], xg_seq[:, width : 2 * width], raw_seq, b_rows, c_rows, rate_own[sl], gain_own[sl]
        )
        x_parts.append(
            lax.all_to_all(x_back, "ctx", split_axis=0, concat_axis=1, tiled=True).reshape(rows, owners, 1, width)
        )
        raw_parts.append(
            lax.all_to_all(raw_back, "ctx", split_axis=0, concat_axis=1, tiled=True).reshape(rows, owners, 1, per_chunk)
        )
        grad_b_all = gb if grad_b_all is None else grad_b_all + gb
        grad_c_all = gc if grad_c_all is None else grad_c_all + gc
    grad_x = jnp.concatenate(x_parts, axis=2).reshape(rows, owners * per_owner * head_width)
    grad_dt = jnp.concatenate(raw_parts, axis=2).reshape(rows, heads_here)

    is_first = half == 0
    send = jnp.where(is_first, grad_c_all, grad_b_all)
    keep = jnp.where(is_first, grad_b_all, grad_c_all)
    mine = keep + lax.ppermute(send, "tp", [(0, 1), (1, 0)])
    parts = lax.all_to_all(mine.reshape(owners, rows, state), "ctx", split_axis=0, concat_axis=0, tiled=True)
    mine = parts.sum(axis=0)
    other = lax.ppermute(mine, "tp", [(0, 1), (1, 0)])
    grad_b = jnp.where(is_first, mine, other)
    grad_c = jnp.where(is_first, other, mine)
    return (grad_x, grad_b, grad_c, grad_dt)


def solution(mesh):
    in_specs = (
        P("ctx", "tp"),
        P("ctx", None),
        P("ctx", None),
        P("ctx", "tp"),
        P("tp"),
        P("tp"),
        P("ctx", "tp"),
    )
    out_specs = (P("ctx", "tp"), P("ctx", None), P("ctx", None), P("ctx", "tp"))
    return jax.shard_map(local, mesh=mesh, in_specs=in_specs, out_specs=out_specs, check_vma=False)
```

```python
from functools import partial

import jax
import jax.numpy as jnp
from jax import lax
from jax.sharding import PartitionSpec as P

BLOCK = 256


precise = lax.Precision.HIGH


def head_forward(x_head, b_rows, c_rows, raw_step, log_rate, skip_gain, start_state, block_len):
    length, head_width = x_head.shape
    blocks = length // block_len
    step_size = jax.nn.softplus(raw_step)
    decay_rates = -jnp.exp(log_rate) * step_size
    row_index = lax.broadcasted_iota(jnp.int32, (block_len, block_len), 0)
    col_index = lax.broadcasted_iota(jnp.int32, (block_len, block_len), 1)
    lower_mask = row_index >= col_index
    running = jnp.dot(
        decay_rates.reshape(blocks, block_len), lower_mask.astype(jnp.float32).T, precision=precise
    )
    between = jnp.where(lower_mask[None], running[:, :, None] - running[:, None, :], -1e30)
    x_blocks = x_head.reshape(blocks, block_len, head_width)
    b_blocks = b_rows.reshape(blocks, block_len, -1)
    c_blocks = c_rows.reshape(blocks, block_len, -1)
    s_blocks = step_size.reshape(blocks, block_len)
    scores = (
        jnp.einsum("kin,kjn->kij", c_blocks, b_blocks, precision=precise)
        * jnp.exp(between)
        * s_blocks[:, None, :]
    )
    output = jnp.einsum("kij,kjp->kip", scores, x_blocks, precision=precise)
    closing = running[:, -1]
    weighted = (jnp.exp(closing[:, None] - running) * s_blocks)[:, :, None] * x_blocks
    states = jnp.einsum("kjp,kjn->kpn", weighted, b_blocks, precision=precise)
    block_rows = lax.broadcasted_iota(jnp.int32, (blocks, blocks), 0)
    block_cols = lax.broadcasted_iota(jnp.int32, (blocks, blocks), 1)
    through = jnp.dot((block_rows >= block_cols).astype(jnp.float32), closing, precision=precise)
    before = through - closing
    carry_weight = jnp.exp(
        jnp.where(block_rows > block_cols, before[:, None] - through[None, :], -1e30)
    )
    entering = (
        jnp.einsum("kj,jpn->kpn", carry_weight, states, precision=precise)
        + jnp.exp(before)[:, None, None] * start_state[None]
    )
    reading = jnp.exp(running)[:, :, None] * c_blocks
    output = output + jnp.einsum("kin,kpn->kip", reading, entering, precision=precise)
    output = output.reshape(length, head_width) + skip_gain * x_head
    final_state = (
        jnp.einsum("j,jpn->pn", jnp.exp(through[-1] - through), states, precision=precise)
        + jnp.exp(through[-1]) * start_state
    )
    return (output, final_state)


N_CHUNKS = 1


def chunk_backward(x_seq, g_seq, raw_seq, b_rows, c_rows, rate, gain):
    length = x_seq.shape[0]
    heads = raw_seq.shape[1]
    head_width = x_seq.shape[1] // heads
    runner = partial(head_forward, block_len=BLOCK)
    mapped = jax.vmap(runner, in_axes=(0, None, None, 0, 0, 0, 0))
    x_heads = x_seq.astype(jnp.float32).reshape(length, heads, head_width).transpose(1, 0, 2)
    g_heads = g_seq.astype(jnp.float32).reshape(length, heads, head_width).transpose(1, 0, 2)
    raw_heads = raw_seq.astype(jnp.float32).T
    anchor = jnp.zeros((heads, head_width, b_rows.shape[1]), jnp.float32)

    def forward(x_val, b_val, c_val, raw_val):
        return mapped(x_val, b_val, c_val, raw_val, rate, gain, anchor)[0]

    _, pullback = jax.vjp(forward, x_heads, b_rows, c_rows, raw_heads)
    grad_xh, grad_b_all, grad_c_all, grad_raw = pullback(g_heads)
    x_back = grad_xh.transpose(1, 0, 2).reshape(length, heads * head_width).astype(jnp.bfloat16)
    raw_back = grad_raw.T.astype(jnp.bfloat16)
    return x_back, raw_back, grad_b_all, grad_c_all


def gather_ctx(block, owners, me):
    if owners & (owners - 1):
        return lax.all_gather(block, "ctx", axis=0, tiled=True)
    have = block
    step = 1
    while step < owners:
        theirs = lax.ppermute(have, "ctx", [(k, k ^ step) for k in range(owners)])
        upper = (me // step) % 2 == 1
        have = jnp.where(upper, jnp.concatenate([theirs, have]), jnp.concatenate([have, theirs]))
        step *= 2
    return have


def local(x_act, b_proj, c_proj, dt_raw, a_log, d_skip, grad_out):
    rows = x_act.shape[0]
    heads_here = dt_raw.shape[1]
    head_width = x_act.shape[1] // heads_here
    state = b_proj.shape[1]
    owners = lax.axis_size("ctx")
    per_owner = heads_here // owners
    chunks = N_CHUNKS if per_owner % N_CHUNKS == 0 else 1
    per_chunk = per_owner // chunks
    me = lax.axis_index("ctx")
    half = lax.axis_index("tp")

    own_seq = gather_ctx(jnp.where(half == 0, b_proj, c_proj), owners, me)
    other_seq = lax.ppermute(own_seq, "tp", [(0, 1), (1, 0)])
    b_rows = jnp.where(half == 0, own_seq, other_seq).astype(jnp.float32)
    c_rows = jnp.where(half == 0, other_seq, own_seq).astype(jnp.float32)
    first_head = me * per_owner
    rate_own = lax.dynamic_slice_in_dim(a_log, first_head, per_owner)
    gain_own = lax.dynamic_slice_in_dim(d_skip, first_head, per_owner)

    x4 = x_act.reshape(rows, owners, per_owner, head_width)
    g4 = grad_out.reshape(rows, owners, per_owner, head_width)
    r3 = dt_raw.reshape(rows, owners, per_owner)
    x_parts, raw_parts = [], []
    grad_b_all = None
    grad_c_all = None
    for c in range(chunks):
        sl = slice(c * per_chunk, (c + 1) * per_chunk)
        width = per_chunk * head_width
        pieces = [x4[:, :, sl, :].reshape(rows, owners, width), g4[:, :, sl, :].reshape(rows, owners, width)]
        xg = jnp.concatenate(pieces, axis=2)
        xg_seq = lax.all_to_all(xg, "ctx", split_axis=1, concat_axis=0, tiled=True).reshape(rows * owners, -1)
        raw_seq = lax.all_to_all(r3[:, :, sl], "ctx", split_axis=1, concat_axis=0, tiled=True).reshape(
            rows * owners, per_chunk
        )
        x_back, raw_back, gb, gc = chunk_backward(
            xg_seq[:, :width], xg_seq[:, width : 2 * width], raw_seq, b_rows, c_rows, rate_own[sl], gain_own[sl]
        )
        x_parts.append(
            lax.all_to_all(x_back, "ctx", split_axis=0, concat_axis=1, tiled=True).reshape(rows, owners, 1, width)
        )
        raw_parts.append(
            lax.all_to_all(raw_back, "ctx", split_axis=0, concat_axis=1, tiled=True).reshape(rows, owners, 1, per_chunk)
        )
        grad_b_all = gb if grad_b_all is None else grad_b_all + gb
        grad_c_all = gc if grad_c_all is None else grad_c_all + gc
    grad_x = jnp.concatenate(x_parts, axis=2).reshape(rows, owners * per_owner * head_width)
    grad_dt = jnp.concatenate(raw_parts, axis=2).reshape(rows, heads_here)

    is_first = half == 0
    send = jnp.where(is_first, grad_c_all, grad_b_all)
    keep = jnp.where(is_first, grad_b_all, grad_c_all)
    mine = keep + lax.ppermute(send, "tp", [(0, 1), (1, 0)])
    parts = lax.all_to_all(mine.reshape(owners, rows, state), "ctx", split_axis=0, concat_axis=0, tiled=True)
    mine = parts.sum(axis=0)
    other = lax.ppermute(mine, "tp", [(0, 1), (1, 0)])
    grad_b = jnp.where(is_first, mine, other)
    grad_c = jnp.where(is_first, other, mine)
    return (grad_x, grad_b, grad_c, grad_dt)


def solution(mesh):
    in_specs = (
        P("ctx", "tp"),
        P("ctx", None),
        P("ctx", None),
        P("ctx", "tp"),
        P("tp"),
        P("tp"),
        P("ctx", "tp"),
    )
    out_specs = (P("ctx", "tp"), P("ctx", None), P("ctx", None), P("ctx", "tp"))
    return jax.shard_map(local, mesh=mesh, in_specs=in_specs, out_specs=out_specs, check_vma=False)
```

```python
from functools import partial

import jax
import jax.numpy as jnp
from jax import lax
from jax.sharding import PartitionSpec as P

BLOCK = 256


precise = lax.Precision.HIGH


def head_forward(x_head, b_rows, c_rows, raw_step, log_rate, skip_gain, start_state, block_len):
    length, head_width = x_head.shape
    blocks = length // block_len
    step_size = jax.nn.softplus(raw_step)
    decay_rates = -jnp.exp(log_rate) * step_size
    row_index = lax.broadcasted_iota(jnp.int32, (block_len, block_len), 0)
    col_index = lax.broadcasted_iota(jnp.int32, (block_len, block_len), 1)
    lower_mask = row_index >= col_index
    running = jnp.dot(
        decay_rates.reshape(blocks, block_len), lower_mask.astype(jnp.float32).T, precision=precise
    )
    between = jnp.where(lower_mask[None], running[:, :, None] - running[:, None, :], -1e30)
    x_blocks = x_head.reshape(blocks, block_len, head_width)
    b_blocks = b_rows.reshape(blocks, block_len, -1)
    c_blocks = c_rows.reshape(blocks, block_len, -1)
    s_blocks = step_size.reshape(blocks, block_len)
    scores = (
        jnp.einsum("kin,kjn->kij", c_blocks, b_blocks, precision=precise)
        * jnp.exp(between)
        * s_blocks[:, None, :]
    )
    output = jnp.einsum("kij,kjp->kip", scores, x_blocks, precision=precise)
    closing = running[:, -1]
    weighted = (jnp.exp(closing[:, None] - running) * s_blocks)[:, :, None] * x_blocks
    states = jnp.einsum("kjp,kjn->kpn", weighted, b_blocks, precision=precise)
    block_rows = lax.broadcasted_iota(jnp.int32, (blocks, blocks), 0)
    block_cols = lax.broadcasted_iota(jnp.int32, (blocks, blocks), 1)
    through = jnp.dot((block_rows >= block_cols).astype(jnp.float32), closing, precision=precise)
    before = through - closing
    carry_weight = jnp.exp(
        jnp.where(block_rows > block_cols, before[:, None] - through[None, :], -1e30)
    )
    entering = (
        jnp.einsum("kj,jpn->kpn", carry_weight, states, precision=precise)
        + jnp.exp(before)[:, None, None] * start_state[None]
    )
    reading = jnp.exp(running)[:, :, None] * c_blocks
    output = output + jnp.einsum("kin,kpn->kip", reading, entering, precision=precise)
    output = output.reshape(length, head_width) + skip_gain * x_head
    final_state = (
        jnp.einsum("j,jpn->pn", jnp.exp(through[-1] - through), states, precision=precise)
        + jnp.exp(through[-1]) * start_state
    )
    return (output, final_state)


N_CHUNKS = 1


def chunk_backward(x_seq, g_seq, raw_seq, b_rows, c_rows, rate, gain):
    length = x_seq.shape[0]
    heads = raw_seq.shape[1]
    head_width = x_seq.shape[1] // heads
    runner = partial(head_forward, block_len=BLOCK)
    mapped = jax.vmap(runner, in_axes=(0, None, None, 0, 0, 0, 0))
    x_heads = x_seq.astype(jnp.float32).reshape(length, heads, head_width).transpose(1, 0, 2)
    g_heads = g_seq.astype(jnp.float32).reshape(length, heads, head_width).transpose(1, 0, 2)
    raw_heads = raw_seq.astype(jnp.float32).T
    anchor = jnp.zeros((heads, head_width, b_rows.shape[1]), jnp.float32)

    def forward(x_val, b_val, c_val, raw_val):
        return mapped(x_val, b_val, c_val, raw_val, rate, gain, anchor)[0]

    _, pullback = jax.vjp(forward, x_heads, b_rows, c_rows, raw_heads)
    grad_xh, grad_b_all, grad_c_all, grad_raw = pullback(g_heads)
    x_back = grad_xh.transpose(1, 0, 2).reshape(length, heads * head_width).astype(jnp.bfloat16)
    raw_back = grad_raw.T.astype(jnp.bfloat16)
    return x_back, raw_back, grad_b_all, grad_c_all


def gather_ctx(block, owners, me):
    if owners & (owners - 1):
        return lax.all_gather(block, "ctx", axis=0, tiled=True)
    have = block
    step = 1
    while step < owners:
        theirs = lax.ppermute(have, "ctx", [(k, k ^ step) for k in range(owners)])
        upper = (me // step) % 2 == 1
        have = jnp.where(upper, jnp.concatenate([theirs, have]), jnp.concatenate([have, theirs]))
        step *= 2
    return have


def scatter_sum_ctx(full, owners, me):
    rows = full.shape[0] // owners
    if owners & (owners - 1):
        parts = lax.all_to_all(full.reshape(owners, rows, -1), "ctx", split_axis=0, concat_axis=0, tiled=True)
        return parts.sum(axis=0)
    have = full
    step = owners // 2
    while step >= 1:
        span = step * rows
        upper = (me // step) % 2 == 1
        low, high = have[:span], have[span:]
        keep = jnp.where(upper, high, low)
        send = jnp.where(upper, low, high)
        have = keep + lax.ppermute(send, "ctx", [(k, k ^ step) for k in range(owners)])
        step //= 2
    return have


def local(x_act, b_proj, c_proj, dt_raw, a_log, d_skip, grad_out):
    rows = x_act.shape[0]
    heads_here = dt_raw.shape[1]
    head_width = x_act.shape[1] // heads_here
    state = b_proj.shape[1]
    owners = lax.axis_size("ctx")
    per_owner = heads_here // owners
    chunks = N_CHUNKS if per_owner % N_CHUNKS == 0 else 1
    per_chunk = per_owner // chunks
    me = lax.axis_index("ctx")
    half = lax.axis_index("tp")

    own_seq = gather_ctx(jnp.where(half == 0, b_proj, c_proj), owners, me)
    other_seq = lax.ppermute(own_seq, "tp", [(0, 1), (1, 0)])
    b_rows = jnp.where(half == 0, own_seq, other_seq).astype(jnp.float32)
    c_rows = jnp.where(half == 0, other_seq, own_seq).astype(jnp.float32)
    first_head = me * per_owner
    rate_own = lax.dynamic_slice_in_dim(a_log, first_head, per_owner)
    gain_own = lax.dynamic_slice_in_dim(d_skip, first_head, per_owner)

    x4 = x_act.reshape(rows, owners, per_owner, head_width)
    g4 = grad_out.reshape(rows, owners, per_owner, head_width)
    r3 = dt_raw.reshape(rows, owners, per_owner)
    x_parts, raw_parts = [], []
    grad_b_all = None
    grad_c_all = None
    for c in range(chunks):
        sl = slice(c * per_chunk, (c + 1) * per_chunk)
        width = per_chunk * head_width
        pieces = [x4[:, :, sl, :].reshape(rows, owners, width), g4[:, :, sl, :].reshape(rows, owners, width)]
        xg = jnp.concatenate(pieces, axis=2)
        xg_seq = lax.all_to_all(xg, "ctx", split_axis=1, concat_axis=0, tiled=True).reshape(rows * owners, -1)
        raw_seq = lax.all_to_all(r3[:, :, sl], "ctx", split_axis=1, concat_axis=0, tiled=True).reshape(
            rows * owners, per_chunk
        )
        x_back, raw_back, gb, gc = chunk_backward(
            xg_seq[:, :width], xg_seq[:, width : 2 * width], raw_seq, b_rows, c_rows, rate_own[sl], gain_own[sl]
        )
        x_parts.append(
            lax.all_to_all(x_back, "ctx", split_axis=0, concat_axis=1, tiled=True).reshape(rows, owners, 1, width)
        )
        raw_parts.append(
            lax.all_to_all(raw_back, "ctx", split_axis=0, concat_axis=1, tiled=True).reshape(rows, owners, 1, per_chunk)
        )
        grad_b_all = gb if grad_b_all is None else grad_b_all + gb
        grad_c_all = gc if grad_c_all is None else grad_c_all + gc
    grad_x = jnp.concatenate(x_parts, axis=2).reshape(rows, owners * per_owner * head_width)
    grad_dt = jnp.concatenate(raw_parts, axis=2).reshape(rows, heads_here)

    is_first = half == 0
    send = jnp.where(is_first, grad_c_all, grad_b_all)
    keep = jnp.where(is_first, grad_b_all, grad_c_all)
    mine = keep + lax.ppermute(send, "tp", [(0, 1), (1, 0)])
    mine = scatter_sum_ctx(mine, owners, me)
    other = lax.ppermute(mine, "tp", [(0, 1), (1, 0)])
    grad_b = jnp.where(is_first, mine, other)
    grad_c = jnp.where(is_first, other, mine)
    return (grad_x, grad_b, grad_c, grad_dt)


def solution(mesh):
    in_specs = (
        P("ctx", "tp"),
        P("ctx", None),
        P("ctx", None),
        P("ctx", "tp"),
        P("tp"),
        P("tp"),
        P("ctx", "tp"),
    )
    out_specs = (P("ctx", "tp"), P("ctx", None), P("ctx", None), P("ctx", "tp"))
    return jax.shard_map(local, mesh=mesh, in_specs=in_specs, out_specs=out_specs, check_vma=False)
```

```python
from functools import partial

import jax
import jax.numpy as jnp
from jax import lax
from jax.sharding import PartitionSpec as P

BLOCK = 256


precise = lax.Precision.HIGH


def head_forward(x_head, b_rows, c_rows, raw_step, log_rate, skip_gain, start_state, block_len):
    length, head_width = x_head.shape
    blocks = length // block_len
    step_size = jax.nn.softplus(raw_step)
    decay_rates = -jnp.exp(log_rate) * step_size
    row_index = lax.broadcasted_iota(jnp.int32, (block_len, block_len), 0)
    col_index = lax.broadcasted_iota(jnp.int32, (block_len, block_len), 1)
    lower_mask = row_index >= col_index
    running = jnp.dot(
        decay_rates.reshape(blocks, block_len), lower_mask.astype(jnp.float32).T, precision=precise
    )
    between = jnp.where(lower_mask[None], running[:, :, None] - running[:, None, :], -1e30)
    x_blocks = x_head.reshape(blocks, block_len, head_width)
    b_blocks = b_rows.reshape(blocks, block_len, -1)
    c_blocks = c_rows.reshape(blocks, block_len, -1)
    s_blocks = step_size.reshape(blocks, block_len)
    scores = (
        jnp.einsum("kin,kjn->kij", c_blocks, b_blocks, precision=precise)
        * jnp.exp(between)
        * s_blocks[:, None, :]
    )
    output = jnp.einsum("kij,kjp->kip", scores, x_blocks, precision=precise)
    closing = running[:, -1]
    weighted = (jnp.exp(closing[:, None] - running) * s_blocks)[:, :, None] * x_blocks
    states = jnp.einsum("kjp,kjn->kpn", weighted, b_blocks, precision=precise)
    block_rows = lax.broadcasted_iota(jnp.int32, (blocks, blocks), 0)
    block_cols = lax.broadcasted_iota(jnp.int32, (blocks, blocks), 1)
    through = jnp.dot((block_rows >= block_cols).astype(jnp.float32), closing, precision=precise)
    before = through - closing
    carry_weight = jnp.exp(
        jnp.where(block_rows > block_cols, before[:, None] - through[None, :], -1e30)
    )
    entering = (
        jnp.einsum("kj,jpn->kpn", carry_weight, states, precision=precise)
        + jnp.exp(before)[:, None, None] * start_state[None]
    )
    reading = jnp.exp(running)[:, :, None] * c_blocks
    output = output + jnp.einsum("kin,kpn->kip", reading, entering, precision=precise)
    output = output.reshape(length, head_width) + skip_gain * x_head
    final_state = (
        jnp.einsum("j,jpn->pn", jnp.exp(through[-1] - through), states, precision=precise)
        + jnp.exp(through[-1]) * start_state
    )
    return (output, final_state)


N_CHUNKS = 1


def chunk_backward_autodiff(x_seq, g_seq, raw_seq, b_rows, c_rows, rate, gain):
    length = x_seq.shape[0]
    heads = raw_seq.shape[1]
    head_width = x_seq.shape[1] // heads
    runner = partial(head_forward, block_len=BLOCK)
    mapped = jax.vmap(runner, in_axes=(0, None, None, 0, 0, 0, 0))
    x_heads = x_seq.astype(jnp.float32).reshape(length, heads, head_width).transpose(1, 0, 2)
    g_heads = g_seq.astype(jnp.float32).reshape(length, heads, head_width).transpose(1, 0, 2)
    raw_heads = raw_seq.astype(jnp.float32).T
    anchor = jnp.zeros((heads, head_width, b_rows.shape[1]), jnp.float32)

    def forward(x_val, b_val, c_val, raw_val):
        return mapped(x_val, b_val, c_val, raw_val, rate, gain, anchor)[0]

    _, pullback = jax.vjp(forward, x_heads, b_rows, c_rows, raw_heads)
    grad_xh, grad_b_all, grad_c_all, grad_raw = pullback(g_heads)
    x_back = grad_xh.transpose(1, 0, 2).reshape(length, heads * head_width).astype(jnp.bfloat16)
    raw_back = grad_raw.T.astype(jnp.bfloat16)
    return x_back, raw_back, grad_b_all, grad_c_all


def chunk_backward(x_seq, g_seq, raw_seq, b_rows, c_rows, rate, gain):
    f32 = jnp.float32
    length = x_seq.shape[0]
    heads = raw_seq.shape[1]
    width = x_seq.shape[1] // heads
    span = BLOCK
    blocks = length // span
    state = b_rows.shape[1]
    hi = lax.Precision.HIGH
    x_lo = x_seq.reshape(blocks, span, heads, width).transpose(2, 0, 1, 3)
    g_lo = g_seq.reshape(blocks, span, heads, width).transpose(2, 0, 1, 3)
    x = x_lo.astype(f32)
    g = g_lo.astype(f32)
    raw = raw_seq.astype(f32).T.reshape(heads, blocks, span)
    dt = jax.nn.softplus(raw)
    speed = jnp.exp(rate)
    run = jnp.cumsum(-speed[:, None, None] * dt, axis=-1)
    close = run[..., -1]
    through = jnp.cumsum(close, axis=-1)
    before = through - close
    bb = b_rows.reshape(blocks, span, state)
    cc = c_rows.reshape(blocks, span, state)
    b_lo = bb.astype(jnp.bfloat16)
    c_lo = cc.astype(jnp.bfloat16)
    row_index = lax.broadcasted_iota(jnp.int32, (span, span), 0)
    col_index = lax.broadcasted_iota(jnp.int32, (span, span), 1)
    lower = row_index >= col_index
    decay = jnp.exp(jnp.where(lower, run[..., :, None] - run[..., None, :], -1e30))
    cb = jnp.einsum("kin,kjn->kij", c_lo, b_lo, preferred_element_type=f32)
    gx = jnp.einsum("hkip,hkjp->hkij", g_lo, x_lo, preferred_element_type=f32)
    pm = cb[None] * decay
    wm = gx * decay
    y_in = jnp.einsum("hkij,hkjp->hkip", pm * dt[..., None, :], x, precision=hi)
    q_in = jnp.einsum("hkij,hkip->hkjp", pm, g, precision=hi)
    gc_in = jnp.einsum("hkij,kjn->hkin", wm * dt[..., None, :], bb, precision=hi)
    gb_in = jnp.einsum("hkij,kin->hkjn", wm, cc, precision=hi)
    to_end = jnp.exp(close[..., None] - run)
    from_start = jnp.exp(run)
    s_loc = jnp.einsum("hkjp,kjn->hkpn", (to_end * dt)[..., None] * x, bb, precision=hi)
    r_loc = jnp.einsum("hkip,kin->hkpn", from_start[..., None] * g, cc, precision=hi)
    block_rows = lax.broadcasted_iota(jnp.int32, (blocks, blocks), 0)
    block_cols = lax.broadcasted_iota(jnp.int32, (blocks, blocks), 1)
    carry = jnp.exp(jnp.where(block_rows > block_cols, before[:, :, None] - through[:, None, :], -1e30))
    s_enter = jnp.einsum("hkm,hmpn->hkpn", carry, s_loc, precision=hi)
    r_leave = jnp.einsum("hmk,hmpn->hkpn", carry, r_loc, precision=hi)
    y_out = y_in + from_start[..., None] * jnp.einsum("kin,hkpn->hkip", cc, s_enter, precision=hi)
    gc = gc_in + from_start[..., None] * jnp.einsum("hkip,hkpn->hkin", g, s_enter, precision=hi)
    q = q_in + to_end[..., None] * jnp.einsum("kjn,hkpn->hkjp", bb, r_leave, precision=hi)
    gb = dt[..., None] * (gb_in + to_end[..., None] * jnp.einsum("hkjp,hkpn->hkjn", x, r_leave, precision=hi))
    grad_x = dt[..., None] * q + gain[:, None, None, None] * g
    xq = jnp.sum(x * q, axis=-1)
    d_cum = (jnp.sum(g * y_out, axis=-1) - dt * xq).reshape(heads, length)
    d_decay = jnp.flip(jnp.cumsum(jnp.flip(d_cum, -1), axis=-1), -1).reshape(heads, blocks, span)
    grad_raw = (xq - speed[:, None, None] * d_decay) * jax.nn.sigmoid(raw)
    x_back = grad_x.transpose(1, 2, 0, 3).reshape(length, heads * width).astype(jnp.bfloat16)
    raw_back = grad_raw.reshape(heads, length).T.astype(jnp.bfloat16)
    return x_back, raw_back, gb.sum(0).reshape(length, state), gc.sum(0).reshape(length, state)


def gather_ctx(block, owners, me):
    if owners & (owners - 1):
        return lax.all_gather(block, "ctx", axis=0, tiled=True)
    have = block
    step = 1
    while step < owners:
        theirs = lax.ppermute(have, "ctx", [(k, k ^ step) for k in range(owners)])
        upper = (me // step) % 2 == 1
        have = jnp.where(upper, jnp.concatenate([theirs, have]), jnp.concatenate([have, theirs]))
        step *= 2
    return have


def local(x_act, b_proj, c_proj, dt_raw, a_log, d_skip, grad_out):
    rows = x_act.shape[0]
    heads_here = dt_raw.shape[1]
    head_width = x_act.shape[1] // heads_here
    state = b_proj.shape[1]
    owners = lax.axis_size("ctx")
    per_owner = heads_here // owners
    chunks = N_CHUNKS if per_owner % N_CHUNKS == 0 else 1
    per_chunk = per_owner // chunks
    me = lax.axis_index("ctx")
    half = lax.axis_index("tp")

    own_seq = gather_ctx(jnp.where(half == 0, b_proj, c_proj), owners, me)
    other_seq = lax.ppermute(own_seq, "tp", [(0, 1), (1, 0)])
    b_rows = jnp.where(half == 0, own_seq, other_seq).astype(jnp.float32)
    c_rows = jnp.where(half == 0, other_seq, own_seq).astype(jnp.float32)
    first_head = me * per_owner
    rate_own = lax.dynamic_slice_in_dim(a_log, first_head, per_owner)
    gain_own = lax.dynamic_slice_in_dim(d_skip, first_head, per_owner)

    x4 = x_act.reshape(rows, owners, per_owner, head_width)
    g4 = grad_out.reshape(rows, owners, per_owner, head_width)
    r3 = dt_raw.reshape(rows, owners, per_owner)
    x_parts, raw_parts = [], []
    grad_b_all = None
    grad_c_all = None
    for c in range(chunks):
        sl = slice(c * per_chunk, (c + 1) * per_chunk)
        width = per_chunk * head_width
        pieces = [x4[:, :, sl, :].reshape(rows, owners, width), g4[:, :, sl, :].reshape(rows, owners, width)]
        xg = jnp.concatenate(pieces, axis=2)
        xg_seq = lax.all_to_all(xg, "ctx", split_axis=1, concat_axis=0, tiled=True).reshape(rows * owners, -1)
        raw_seq = lax.all_to_all(r3[:, :, sl], "ctx", split_axis=1, concat_axis=0, tiled=True).reshape(
            rows * owners, per_chunk
        )
        x_back, raw_back, gb, gc = chunk_backward(
            xg_seq[:, :width], xg_seq[:, width : 2 * width], raw_seq, b_rows, c_rows, rate_own[sl], gain_own[sl]
        )
        x_parts.append(
            lax.all_to_all(x_back, "ctx", split_axis=0, concat_axis=1, tiled=True).reshape(rows, owners, 1, width)
        )
        raw_parts.append(
            lax.all_to_all(raw_back, "ctx", split_axis=0, concat_axis=1, tiled=True).reshape(rows, owners, 1, per_chunk)
        )
        grad_b_all = gb if grad_b_all is None else grad_b_all + gb
        grad_c_all = gc if grad_c_all is None else grad_c_all + gc
    grad_x = jnp.concatenate(x_parts, axis=2).reshape(rows, owners * per_owner * head_width)
    grad_dt = jnp.concatenate(raw_parts, axis=2).reshape(rows, heads_here)

    is_first = half == 0
    send = jnp.where(is_first, grad_c_all, grad_b_all)
    keep = jnp.where(is_first, grad_b_all, grad_c_all)
    mine = keep + lax.ppermute(send, "tp", [(0, 1), (1, 0)])
    parts = lax.all_to_all(mine.reshape(owners, rows, state), "ctx", split_axis=0, concat_axis=0, tiled=True)
    mine = parts.sum(axis=0)
    other = lax.ppermute(mine, "tp", [(0, 1), (1, 0)])
    grad_b = jnp.where(is_first, mine, other)
    grad_c = jnp.where(is_first, other, mine)
    return (grad_x, grad_b, grad_c, grad_dt)


def solution(mesh):
    in_specs = (
        P("ctx", "tp"),
        P("ctx", None),
        P("ctx", None),
        P("ctx", "tp"),
        P("tp"),
        P("tp"),
        P("ctx", "tp"),
    )
    out_specs = (P("ctx", "tp"), P("ctx", None), P("ctx", None), P("ctx", "tp"))
    return jax.shard_map(local, mesh=mesh, in_specs=in_specs, out_specs=out_specs, check_vma=False)
```

```python
from functools import partial

import jax
import jax.numpy as jnp
from jax import lax
from jax.sharding import PartitionSpec as P

BLOCK = 256


precise = lax.Precision.HIGH


def head_forward(x_head, b_rows, c_rows, raw_step, log_rate, skip_gain, start_state, block_len):
    length, head_width = x_head.shape
    blocks = length // block_len
    step_size = jax.nn.softplus(raw_step)
    decay_rates = -jnp.exp(log_rate) * step_size
    row_index = lax.broadcasted_iota(jnp.int32, (block_len, block_len), 0)
    col_index = lax.broadcasted_iota(jnp.int32, (block_len, block_len), 1)
    lower_mask = row_index >= col_index
    running = jnp.dot(
        decay_rates.reshape(blocks, block_len), lower_mask.astype(jnp.float32).T, precision=precise
    )
    between = jnp.where(lower_mask[None], running[:, :, None] - running[:, None, :], -1e30)
    x_blocks = x_head.reshape(blocks, block_len, head_width)
    b_blocks = b_rows.reshape(blocks, block_len, -1)
    c_blocks = c_rows.reshape(blocks, block_len, -1)
    s_blocks = step_size.reshape(blocks, block_len)
    scores = (
        jnp.einsum("kin,kjn->kij", c_blocks, b_blocks, precision=precise)
        * jnp.exp(between)
        * s_blocks[:, None, :]
    )
    output = jnp.einsum("kij,kjp->kip", scores, x_blocks, precision=precise)
    closing = running[:, -1]
    weighted = (jnp.exp(closing[:, None] - running) * s_blocks)[:, :, None] * x_blocks
    states = jnp.einsum("kjp,kjn->kpn", weighted, b_blocks, precision=precise)
    block_rows = lax.broadcasted_iota(jnp.int32, (blocks, blocks), 0)
    block_cols = lax.broadcasted_iota(jnp.int32, (blocks, blocks), 1)
    through = jnp.dot((block_rows >= block_cols).astype(jnp.float32), closing, precision=precise)
    before = through - closing
    carry_weight = jnp.exp(
        jnp.where(block_rows > block_cols, before[:, None] - through[None, :], -1e30)
    )
    entering = (
        jnp.einsum("kj,jpn->kpn", carry_weight, states, precision=precise)
        + jnp.exp(before)[:, None, None] * start_state[None]
    )
    reading = jnp.exp(running)[:, :, None] * c_blocks
    output = output + jnp.einsum("kin,kpn->kip", reading, entering, precision=precise)
    output = output.reshape(length, head_width) + skip_gain * x_head
    final_state = (
        jnp.einsum("j,jpn->pn", jnp.exp(through[-1] - through), states, precision=precise)
        + jnp.exp(through[-1]) * start_state
    )
    return (output, final_state)


N_CHUNKS = 2


def chunk_backward(x_seq, g_seq, raw_seq, b_rows, c_rows, rate, gain):
    length = x_seq.shape[0]
    heads = raw_seq.shape[1]
    head_width = x_seq.shape[1] // heads
    runner = partial(head_forward, block_len=BLOCK)
    mapped = jax.vmap(runner, in_axes=(0, None, None, 0, 0, 0, 0))
    x_heads = x_seq.astype(jnp.float32).reshape(length, heads, head_width).transpose(1, 0, 2)
    g_heads = g_seq.astype(jnp.float32).reshape(length, heads, head_width).transpose(1, 0, 2)
    raw_heads = raw_seq.astype(jnp.float32).T
    anchor = jnp.zeros((heads, head_width, b_rows.shape[1]), jnp.float32)

    def forward(x_val, b_val, c_val, raw_val):
        return mapped(x_val, b_val, c_val, raw_val, rate, gain, anchor)[0]

    _, pullback = jax.vjp(forward, x_heads, b_rows, c_rows, raw_heads)
    grad_xh, grad_b_all, grad_c_all, grad_raw = pullback(g_heads)
    x_back = grad_xh.transpose(1, 0, 2).reshape(length, heads * head_width).astype(jnp.bfloat16)
    raw_back = grad_raw.T.astype(jnp.bfloat16)
    return x_back, raw_back, grad_b_all, grad_c_all


def gather_ctx(block, owners, me):
    if owners & (owners - 1):
        return lax.all_gather(block, "ctx", axis=0, tiled=True)
    have = block
    step = 1
    while step < owners:
        theirs = lax.ppermute(have, "ctx", [(k, k ^ step) for k in range(owners)])
        upper = (me // step) % 2 == 1
        have = jnp.where(upper, jnp.concatenate([theirs, have]), jnp.concatenate([have, theirs]))
        step *= 2
    return have


def local(x_act, b_proj, c_proj, dt_raw, a_log, d_skip, grad_out):
    rows = x_act.shape[0]
    heads_here = dt_raw.shape[1]
    head_width = x_act.shape[1] // heads_here
    state = b_proj.shape[1]
    owners = lax.axis_size("ctx")
    per_owner = heads_here // owners
    bounds = [0, 1, per_owner] if per_owner > 1 and N_CHUNKS > 1 else [0, per_owner]
    me = lax.axis_index("ctx")
    half = lax.axis_index("tp")

    own_seq = gather_ctx(jnp.where(half == 0, b_proj, c_proj), owners, me)
    other_seq = lax.ppermute(own_seq, "tp", [(0, 1), (1, 0)])
    b_rows = jnp.where(half == 0, own_seq, other_seq).astype(jnp.float32)
    c_rows = jnp.where(half == 0, other_seq, own_seq).astype(jnp.float32)
    first_head = me * per_owner
    rate_own = lax.dynamic_slice_in_dim(a_log, first_head, per_owner)
    gain_own = lax.dynamic_slice_in_dim(d_skip, first_head, per_owner)

    x4 = x_act.reshape(rows, owners, per_owner, head_width)
    g4 = grad_out.reshape(rows, owners, per_owner, head_width)
    r3 = dt_raw.reshape(rows, owners, per_owner)
    x_parts, raw_parts = [], []
    grad_b_all = None
    grad_c_all = None
    for c in range(len(bounds) - 1):
        sl = slice(bounds[c], bounds[c + 1])
        per_chunk = bounds[c + 1] - bounds[c]
        width = per_chunk * head_width
        pieces = [x4[:, :, sl, :].reshape(rows, owners, width), g4[:, :, sl, :].reshape(rows, owners, width)]
        xg = jnp.concatenate(pieces, axis=2)
        xg_seq = lax.all_to_all(xg, "ctx", split_axis=1, concat_axis=0, tiled=True).reshape(rows * owners, -1)
        raw_seq = lax.all_to_all(r3[:, :, sl], "ctx", split_axis=1, concat_axis=0, tiled=True).reshape(
            rows * owners, per_chunk
        )
        x_back, raw_back, gb, gc = chunk_backward(
            xg_seq[:, :width], xg_seq[:, width : 2 * width], raw_seq, b_rows, c_rows, rate_own[sl], gain_own[sl]
        )
        x_parts.append(
            lax.all_to_all(x_back, "ctx", split_axis=0, concat_axis=1, tiled=True).reshape(rows, owners, width)
        )
        raw_parts.append(
            lax.all_to_all(raw_back, "ctx", split_axis=0, concat_axis=1, tiled=True).reshape(rows, owners, per_chunk)
        )
        grad_b_all = gb if grad_b_all is None else grad_b_all + gb
        grad_c_all = gc if grad_c_all is None else grad_c_all + gc
    grad_x = jnp.concatenate(x_parts, axis=2).reshape(rows, owners * per_owner * head_width)
    grad_dt = jnp.concatenate(raw_parts, axis=2).reshape(rows, heads_here)

    is_first = half == 0
    send = jnp.where(is_first, grad_c_all, grad_b_all)
    keep = jnp.where(is_first, grad_b_all, grad_c_all)
    mine = keep + lax.ppermute(send, "tp", [(0, 1), (1, 0)])
    parts = lax.all_to_all(mine.reshape(owners, rows, state), "ctx", split_axis=0, concat_axis=0, tiled=True)
    mine = parts.sum(axis=0)
    other = lax.ppermute(mine, "tp", [(0, 1), (1, 0)])
    grad_b = jnp.where(is_first, mine, other)
    grad_c = jnp.where(is_first, other, mine)
    return (grad_x, grad_b, grad_c, grad_dt)


def solution(mesh):
    in_specs = (
        P("ctx", "tp"),
        P("ctx", None),
        P("ctx", None),
        P("ctx", "tp"),
        P("tp"),
        P("tp"),
        P("ctx", "tp"),
    )
    out_specs = (P("ctx", "tp"), P("ctx", None), P("ctx", None), P("ctx", "tp"))
    return jax.shard_map(local, mesh=mesh, in_specs=in_specs, out_specs=out_specs, check_vma=False)
```

```python
from functools import partial

import jax
import jax.numpy as jnp
from jax import lax
from jax.sharding import PartitionSpec as P

BLOCK = 256


precise = lax.Precision.HIGH


def head_forward(x_head, b_rows, c_rows, raw_step, log_rate, skip_gain, start_state, block_len):
    length, head_width = x_head.shape
    blocks = length // block_len
    step_size = jax.nn.softplus(raw_step)
    decay_rates = -jnp.exp(log_rate) * step_size
    row_index = lax.broadcasted_iota(jnp.int32, (block_len, block_len), 0)
    col_index = lax.broadcasted_iota(jnp.int32, (block_len, block_len), 1)
    lower_mask = row_index >= col_index
    running = jnp.dot(
        decay_rates.reshape(blocks, block_len), lower_mask.astype(jnp.float32).T, precision=precise
    )
    between = jnp.where(lower_mask[None], running[:, :, None] - running[:, None, :], -1e30)
    x_blocks = x_head.reshape(blocks, block_len, head_width)
    b_blocks = b_rows.reshape(blocks, block_len, -1)
    c_blocks = c_rows.reshape(blocks, block_len, -1)
    s_blocks = step_size.reshape(blocks, block_len)
    scores = (
        jnp.einsum("kin,kjn->kij", c_blocks, b_blocks, precision=precise)
        * jnp.exp(between)
        * s_blocks[:, None, :]
    )
    output = jnp.einsum("kij,kjp->kip", scores, x_blocks, precision=precise)
    closing = running[:, -1]
    weighted = (jnp.exp(closing[:, None] - running) * s_blocks)[:, :, None] * x_blocks
    states = jnp.einsum("kjp,kjn->kpn", weighted, b_blocks, precision=precise)
    block_rows = lax.broadcasted_iota(jnp.int32, (blocks, blocks), 0)
    block_cols = lax.broadcasted_iota(jnp.int32, (blocks, blocks), 1)
    through = jnp.dot((block_rows >= block_cols).astype(jnp.float32), closing, precision=precise)
    before = through - closing
    carry_weight = jnp.exp(
        jnp.where(block_rows > block_cols, before[:, None] - through[None, :], -1e30)
    )
    entering = (
        jnp.einsum("kj,jpn->kpn", carry_weight, states, precision=precise)
        + jnp.exp(before)[:, None, None] * start_state[None]
    )
    reading = jnp.exp(running)[:, :, None] * c_blocks
    output = output + jnp.einsum("kin,kpn->kip", reading, entering, precision=precise)
    output = output.reshape(length, head_width) + skip_gain * x_head
    final_state = (
        jnp.einsum("j,jpn->pn", jnp.exp(through[-1] - through), states, precision=precise)
        + jnp.exp(through[-1]) * start_state
    )
    return (output, final_state)


def chunk_backward(x_seq, g_seq, raw_seq, b_rows, c_rows, rate, gain):
    length = x_seq.shape[0]
    heads = raw_seq.shape[1]
    head_width = x_seq.shape[1] // heads
    runner = partial(head_forward, block_len=BLOCK)
    mapped = jax.vmap(runner, in_axes=(0, None, None, 0, 0, 0, 0))
    x_heads = x_seq.astype(jnp.float32).reshape(length, heads, head_width).transpose(1, 0, 2)
    g_heads = g_seq.astype(jnp.float32).reshape(length, heads, head_width).transpose(1, 0, 2)
    raw_heads = raw_seq.astype(jnp.float32).T
    anchor = jnp.zeros((heads, head_width, b_rows.shape[1]), jnp.float32)

    def forward(x_val, b_val, c_val, raw_val):
        return mapped(x_val, b_val, c_val, raw_val, rate, gain, anchor)[0]

    _, pullback = jax.vjp(forward, x_heads, b_rows, c_rows, raw_heads)
    grad_xh, grad_b_all, grad_c_all, grad_raw = pullback(g_heads)
    x_back = grad_xh.transpose(1, 0, 2).reshape(length, heads * head_width).astype(jnp.bfloat16)
    raw_back = grad_raw.T.astype(jnp.bfloat16)
    return x_back, raw_back, grad_b_all, grad_c_all


def gather_ctx(block, owners, me):
    if owners & (owners - 1):
        return lax.all_gather(block, "ctx", axis=0, tiled=True)
    have = block
    step = 1
    while step < owners:
        theirs = lax.ppermute(have, "ctx", [(k, k ^ step) for k in range(owners)])
        upper = (me // step) % 2 == 1
        have = jnp.where(upper, jnp.concatenate([theirs, have]), jnp.concatenate([have, theirs]))
        step *= 2
    return have


def local(x_act, b_proj, c_proj, dt_raw, a_log, d_skip, grad_out):
    rows = x_act.shape[0]
    heads_here = dt_raw.shape[1]
    head_width = x_act.shape[1] // heads_here
    state = b_proj.shape[1]
    owners = lax.axis_size("ctx")
    per_owner = heads_here // owners
    width = per_owner * head_width
    me = lax.axis_index("ctx")
    half = lax.axis_index("tp")
    is_first = half == 0

    own_seq = gather_ctx(jnp.where(is_first, b_proj, c_proj), owners, me)
    other_seq = lax.ppermute(own_seq, "tp", [(0, 1), (1, 0)])
    b_rows = jnp.where(is_first, own_seq, other_seq).astype(jnp.float32)
    c_rows = jnp.where(is_first, other_seq, own_seq).astype(jnp.float32)
    first_head = me * per_owner
    rate_own = lax.dynamic_slice_in_dim(a_log, first_head, per_owner)
    gain_own = lax.dynamic_slice_in_dim(d_skip, first_head, per_owner)

    xg = jnp.concatenate(
        [x_act.reshape(rows, owners, width), grad_out.reshape(rows, owners, width)], axis=2
    ).transpose(1, 0, 2)
    steps = dt_raw.reshape(rows, owners, per_owner).transpose(1, 2, 0)
    extra_in = (per_owner * rows) // (2 * width)
    fold_in = extra_in * 2 * width == per_owner * rows
    if fold_in:
        packed = jnp.concatenate([xg, steps.reshape(owners, extra_in, 2 * width)], axis=1)
        got = lax.all_to_all(packed, "ctx", split_axis=0, concat_axis=0, tiled=True)
        xg_seq = got[:, :rows, :].reshape(owners * rows, 2 * width)
        raw_seq = got[:, rows:, :].reshape(owners, per_owner, rows).transpose(0, 2, 1)
    else:
        xg_seq = lax.all_to_all(xg, "ctx", split_axis=0, concat_axis=0, tiled=True).reshape(owners * rows, -1)
        raw_seq = lax.all_to_all(steps, "ctx", split_axis=0, concat_axis=0, tiled=True).transpose(0, 2, 1)
    raw_seq = raw_seq.reshape(owners * rows, per_owner)

    x_back, raw_back, grad_b_all, grad_c_all = chunk_backward(
        xg_seq[:, :width], xg_seq[:, width:], raw_seq, b_rows, c_rows, rate_own, gain_own
    )

    back = x_back.reshape(owners, rows, width)
    steps_back = raw_back.reshape(owners, rows, per_owner).transpose(0, 2, 1)
    extra_out = (per_owner * rows) // width
    if extra_out * width == per_owner * rows:
        packed = jnp.concatenate([back, steps_back.reshape(owners, extra_out, width)], axis=1)
        got = lax.all_to_all(packed, "ctx", split_axis=0, concat_axis=0, tiled=True)
        got_x = got[:, :rows, :]
        got_dt = got[:, rows:, :].reshape(owners, per_owner, rows)
    else:
        got_x = lax.all_to_all(back, "ctx", split_axis=0, concat_axis=0, tiled=True)
        got_dt = lax.all_to_all(steps_back, "ctx", split_axis=0, concat_axis=0, tiled=True)
    grad_x = got_x.transpose(1, 0, 2).reshape(rows, owners * width)
    grad_dt = got_dt.transpose(2, 0, 1).reshape(rows, heads_here)

    send = jnp.where(is_first, grad_c_all, grad_b_all)
    keep = jnp.where(is_first, grad_b_all, grad_c_all)
    mine = keep + lax.ppermute(send, "tp", [(0, 1), (1, 0)])
    parts = lax.all_to_all(mine.reshape(owners, rows, state), "ctx", split_axis=0, concat_axis=0, tiled=True)
    mine = parts.sum(axis=0)
    other = lax.ppermute(mine, "tp", [(0, 1), (1, 0)])
    grad_b = jnp.where(is_first, mine, other)
    grad_c = jnp.where(is_first, other, mine)
    return (grad_x, grad_b, grad_c, grad_dt)


def solution(mesh):
    in_specs = (
        P("ctx", "tp"),
        P("ctx", None),
        P("ctx", None),
        P("ctx", "tp"),
        P("tp"),
        P("tp"),
        P("ctx", "tp"),
    )
    out_specs = (P("ctx", "tp"), P("ctx", None), P("ctx", None), P("ctx", "tp"))
    return jax.shard_map(local, mesh=mesh, in_specs=in_specs, out_specs=out_specs, check_vma=False)
```

```python
from functools import partial

import jax
import jax.numpy as jnp
from jax import lax
from jax.sharding import PartitionSpec as P

BLOCK = 256


precise = lax.Precision.HIGH


def head_forward(x_head, b_rows, c_rows, raw_step, log_rate, skip_gain, start_state, block_len):
    length, head_width = x_head.shape
    blocks = length // block_len
    step_size = jax.nn.softplus(raw_step)
    decay_rates = -jnp.exp(log_rate) * step_size
    row_index = lax.broadcasted_iota(jnp.int32, (block_len, block_len), 0)
    col_index = lax.broadcasted_iota(jnp.int32, (block_len, block_len), 1)
    lower_mask = row_index >= col_index
    running = jnp.dot(
        decay_rates.reshape(blocks, block_len), lower_mask.astype(jnp.float32).T, precision=precise
    )
    between = jnp.where(lower_mask[None], running[:, :, None] - running[:, None, :], -1e30)
    x_blocks = x_head.reshape(blocks, block_len, head_width)
    b_blocks = b_rows.reshape(blocks, block_len, -1)
    c_blocks = c_rows.reshape(blocks, block_len, -1)
    s_blocks = step_size.reshape(blocks, block_len)
    scores = (
        jnp.einsum("kin,kjn->kij", c_blocks, b_blocks, precision=precise)
        * jnp.exp(between)
        * s_blocks[:, None, :]
    )
    output = jnp.einsum("kij,kjp->kip", scores, x_blocks, precision=precise)
    closing = running[:, -1]
    weighted = (jnp.exp(closing[:, None] - running) * s_blocks)[:, :, None] * x_blocks
    states = jnp.einsum("kjp,kjn->kpn", weighted, b_blocks, precision=precise)
    block_rows = lax.broadcasted_iota(jnp.int32, (blocks, blocks), 0)
    block_cols = lax.broadcasted_iota(jnp.int32, (blocks, blocks), 1)
    through = jnp.dot((block_rows >= block_cols).astype(jnp.float32), closing, precision=precise)
    before = through - closing
    carry_weight = jnp.exp(
        jnp.where(block_rows > block_cols, before[:, None] - through[None, :], -1e30)
    )
    entering = (
        jnp.einsum("kj,jpn->kpn", carry_weight, states, precision=precise)
        + jnp.exp(before)[:, None, None] * start_state[None]
    )
    reading = jnp.exp(running)[:, :, None] * c_blocks
    output = output + jnp.einsum("kin,kpn->kip", reading, entering, precision=precise)
    output = output.reshape(length, head_width) + skip_gain * x_head
    final_state = (
        jnp.einsum("j,jpn->pn", jnp.exp(through[-1] - through), states, precision=precise)
        + jnp.exp(through[-1]) * start_state
    )
    return (output, final_state)


N_CHUNKS = 1


def chunk_backward_autodiff(x_seq, g_seq, raw_seq, b_rows, c_rows, rate, gain):
    length = x_seq.shape[0]
    heads = raw_seq.shape[1]
    head_width = x_seq.shape[1] // heads
    runner = partial(head_forward, block_len=BLOCK)
    mapped = jax.vmap(runner, in_axes=(0, None, None, 0, 0, 0, 0))
    x_heads = x_seq.astype(jnp.float32).reshape(length, heads, head_width).transpose(1, 0, 2)
    g_heads = g_seq.astype(jnp.float32).reshape(length, heads, head_width).transpose(1, 0, 2)
    raw_heads = raw_seq.astype(jnp.float32).T
    anchor = jnp.zeros((heads, head_width, b_rows.shape[1]), jnp.float32)

    def forward(x_val, b_val, c_val, raw_val):
        return mapped(x_val, b_val, c_val, raw_val, rate, gain, anchor)[0]

    _, pullback = jax.vjp(forward, x_heads, b_rows, c_rows, raw_heads)
    grad_xh, grad_b_all, grad_c_all, grad_raw = pullback(g_heads)
    x_back = grad_xh.transpose(1, 0, 2).reshape(length, heads * head_width).astype(jnp.bfloat16)
    raw_back = grad_raw.T.astype(jnp.bfloat16)
    return x_back, raw_back, grad_b_all, grad_c_all


def split_dot(spec, wide, narrow):
    top_wide = lax.reduce_precision(wide, exponent_bits=8, mantissa_bits=7)
    top = top_wide.astype(jnp.bfloat16)
    rest = (wide - top_wide).astype(jnp.bfloat16)
    return jnp.einsum(spec, top, narrow, preferred_element_type=jnp.float32) + jnp.einsum(
        spec, rest, narrow, preferred_element_type=jnp.float32
    )


def chunk_backward(x_seq, g_seq, raw_seq, b_rows, c_rows, rate, gain):
    f32 = jnp.float32
    length = x_seq.shape[0]
    heads = raw_seq.shape[1]
    width = x_seq.shape[1] // heads
    span = BLOCK
    blocks = length // span
    state = b_rows.shape[1]
    hi = lax.Precision.HIGH
    x_lo = x_seq.reshape(blocks, span, heads, width).transpose(2, 0, 1, 3)
    g_lo = g_seq.reshape(blocks, span, heads, width).transpose(2, 0, 1, 3)
    x = x_lo.astype(f32)
    g = g_lo.astype(f32)
    raw = raw_seq.astype(f32).T.reshape(heads, blocks, span)
    dt = jax.nn.softplus(raw)
    speed = jnp.exp(rate)
    run = jnp.cumsum(-speed[:, None, None] * dt, axis=-1)
    close = run[..., -1]
    through = jnp.cumsum(close, axis=-1)
    before = through - close
    bb = b_rows.reshape(blocks, span, state)
    cc = c_rows.reshape(blocks, span, state)
    b_lo = bb.astype(jnp.bfloat16)
    c_lo = cc.astype(jnp.bfloat16)
    row_index = lax.broadcasted_iota(jnp.int32, (span, span), 0)
    col_index = lax.broadcasted_iota(jnp.int32, (span, span), 1)
    lower = row_index >= col_index
    decay = jnp.exp(jnp.where(lower, run[..., :, None] - run[..., None, :], -1e30))
    cb = jnp.einsum("kin,kjn->kij", c_lo, b_lo, preferred_element_type=f32)
    gx = jnp.einsum("hkip,hkjp->hkij", g_lo, x_lo, preferred_element_type=f32)
    pm = cb[None] * decay
    wm = gx * decay
    y_in = split_dot("hkij,hkjp->hkip", pm * dt[..., None, :], x_lo)
    q_in = split_dot("hkij,hkip->hkjp", pm, g_lo)
    gc_in = split_dot("hkij,kjn->hkin", wm * dt[..., None, :], b_lo)
    gb_in = split_dot("hkij,kin->hkjn", wm, c_lo)
    to_end = jnp.exp(close[..., None] - run)
    from_start = jnp.exp(run)
    s_loc = jnp.einsum("hkjp,kjn->hkpn", (to_end * dt)[..., None] * x, bb, precision=hi)
    r_loc = jnp.einsum("hkip,kin->hkpn", from_start[..., None] * g, cc, precision=hi)
    block_rows = lax.broadcasted_iota(jnp.int32, (blocks, blocks), 0)
    block_cols = lax.broadcasted_iota(jnp.int32, (blocks, blocks), 1)
    carry = jnp.exp(jnp.where(block_rows > block_cols, before[:, :, None] - through[:, None, :], -1e30))
    s_enter = jnp.einsum("hkm,hmpn->hkpn", carry, s_loc, precision=hi)
    r_leave = jnp.einsum("hmk,hmpn->hkpn", carry, r_loc, precision=hi)
    y_out = y_in + from_start[..., None] * jnp.einsum("kin,hkpn->hkip", cc, s_enter, precision=hi)
    gc = gc_in + from_start[..., None] * jnp.einsum("hkip,hkpn->hkin", g, s_enter, precision=hi)
    q = q_in + to_end[..., None] * jnp.einsum("kjn,hkpn->hkjp", bb, r_leave, precision=hi)
    gb = dt[..., None] * (gb_in + to_end[..., None] * jnp.einsum("hkjp,hkpn->hkjn", x, r_leave, precision=hi))
    grad_x = dt[..., None] * q + gain[:, None, None, None] * g
    xq = jnp.sum(x * q, axis=-1)
    d_cum = (jnp.sum(g * y_out, axis=-1) - dt * xq).reshape(heads, length)
    d_decay = jnp.flip(jnp.cumsum(jnp.flip(d_cum, -1), axis=-1), -1).reshape(heads, blocks, span)
    grad_raw = (xq - speed[:, None, None] * d_decay) * jax.nn.sigmoid(raw)
    x_back = grad_x.transpose(1, 2, 0, 3).reshape(length, heads * width).astype(jnp.bfloat16)
    raw_back = grad_raw.reshape(heads, length).T.astype(jnp.bfloat16)
    return x_back, raw_back, gb.sum(0).reshape(length, state), gc.sum(0).reshape(length, state)


def gather_ctx(block, owners, me):
    if owners & (owners - 1):
        return lax.all_gather(block, "ctx", axis=0, tiled=True)
    have = block
    step = 1
    while step < owners:
        theirs = lax.ppermute(have, "ctx", [(k, k ^ step) for k in range(owners)])
        upper = (me // step) % 2 == 1
        have = jnp.where(upper, jnp.concatenate([theirs, have]), jnp.concatenate([have, theirs]))
        step *= 2
    return have


def local(x_act, b_proj, c_proj, dt_raw, a_log, d_skip, grad_out):
    rows = x_act.shape[0]
    heads_here = dt_raw.shape[1]
    head_width = x_act.shape[1] // heads_here
    state = b_proj.shape[1]
    owners = lax.axis_size("ctx")
    per_owner = heads_here // owners
    chunks = N_CHUNKS if per_owner % N_CHUNKS == 0 else 1
    per_chunk = per_owner // chunks
    me = lax.axis_index("ctx")
    half = lax.axis_index("tp")

    own_seq = gather_ctx(jnp.where(half == 0, b_proj, c_proj), owners, me)
    other_seq = lax.ppermute(own_seq, "tp", [(0, 1), (1, 0)])
    b_rows = jnp.where(half == 0, own_seq, other_seq).astype(jnp.float32)
    c_rows = jnp.where(half == 0, other_seq, own_seq).astype(jnp.float32)
    first_head = me * per_owner
    rate_own = lax.dynamic_slice_in_dim(a_log, first_head, per_owner)
    gain_own = lax.dynamic_slice_in_dim(d_skip, first_head, per_owner)

    x4 = x_act.reshape(rows, owners, per_owner, head_width)
    g4 = grad_out.reshape(rows, owners, per_owner, head_width)
    r3 = dt_raw.reshape(rows, owners, per_owner)
    x_parts, raw_parts = [], []
    grad_b_all = None
    grad_c_all = None
    for c in range(chunks):
        sl = slice(c * per_chunk, (c + 1) * per_chunk)
        width = per_chunk * head_width
        pieces = [x4[:, :, sl, :].reshape(rows, owners, width), g4[:, :, sl, :].reshape(rows, owners, width)]
        xg = jnp.concatenate(pieces, axis=2)
        xg_seq = lax.all_to_all(xg, "ctx", split_axis=1, concat_axis=0, tiled=True).reshape(rows * owners, -1)
        raw_seq = lax.all_to_all(r3[:, :, sl], "ctx", split_axis=1, concat_axis=0, tiled=True).reshape(
            rows * owners, per_chunk
        )
        x_back, raw_back, gb, gc = chunk_backward(
            xg_seq[:, :width], xg_seq[:, width : 2 * width], raw_seq, b_rows, c_rows, rate_own[sl], gain_own[sl]
        )
        x_parts.append(
            lax.all_to_all(x_back, "ctx", split_axis=0, concat_axis=1, tiled=True).reshape(rows, owners, 1, width)
        )
        raw_parts.append(
            lax.all_to_all(raw_back, "ctx", split_axis=0, concat_axis=1, tiled=True).reshape(rows, owners, 1, per_chunk)
        )
        grad_b_all = gb if grad_b_all is None else grad_b_all + gb
        grad_c_all = gc if grad_c_all is None else grad_c_all + gc
    grad_x = jnp.concatenate(x_parts, axis=2).reshape(rows, owners * per_owner * head_width)
    grad_dt = jnp.concatenate(raw_parts, axis=2).reshape(rows, heads_here)

    is_first = half == 0
    send = jnp.where(is_first, grad_c_all, grad_b_all)
    keep = jnp.where(is_first, grad_b_all, grad_c_all)
    mine = keep + lax.ppermute(send, "tp", [(0, 1), (1, 0)])
    parts = lax.all_to_all(mine.reshape(owners, rows, state), "ctx", split_axis=0, concat_axis=0, tiled=True)
    mine = parts.sum(axis=0)
    other = lax.ppermute(mine, "tp", [(0, 1), (1, 0)])
    grad_b = jnp.where(is_first, mine, other)
    grad_c = jnp.where(is_first, other, mine)
    return (grad_x, grad_b, grad_c, grad_dt)


def solution(mesh):
    in_specs = (
        P("ctx", "tp"),
        P("ctx", None),
        P("ctx", None),
        P("ctx", "tp"),
        P("tp"),
        P("tp"),
        P("ctx", "tp"),
    )
    out_specs = (P("ctx", "tp"), P("ctx", None), P("ctx", None), P("ctx", "tp"))
    return jax.shard_map(local, mesh=mesh, in_specs=in_specs, out_specs=out_specs, check_vma=False)
```

```python
from functools import partial

import jax
import jax.numpy as jnp
from jax import lax
from jax.sharding import PartitionSpec as P

BLOCK = 256


precise = lax.Precision.HIGH


def head_forward(x_head, b_rows, c_rows, raw_step, log_rate, skip_gain, start_state, block_len):
    length, head_width = x_head.shape
    blocks = length // block_len
    step_size = jax.nn.softplus(raw_step)
    decay_rates = -jnp.exp(log_rate) * step_size
    row_index = lax.broadcasted_iota(jnp.int32, (block_len, block_len), 0)
    col_index = lax.broadcasted_iota(jnp.int32, (block_len, block_len), 1)
    lower_mask = row_index >= col_index
    running = jnp.dot(
        decay_rates.reshape(blocks, block_len), lower_mask.astype(jnp.float32).T, precision=precise
    )
    between = jnp.where(lower_mask[None], running[:, :, None] - running[:, None, :], -1e30)
    x_blocks = x_head.reshape(blocks, block_len, head_width)
    b_blocks = b_rows.reshape(blocks, block_len, -1)
    c_blocks = c_rows.reshape(blocks, block_len, -1)
    s_blocks = step_size.reshape(blocks, block_len)
    scores = (
        jnp.einsum("kin,kjn->kij", c_blocks, b_blocks, precision=precise)
        * jnp.exp(between)
        * s_blocks[:, None, :]
    )
    output = jnp.einsum("kij,kjp->kip", scores, x_blocks, precision=precise)
    closing = running[:, -1]
    weighted = (jnp.exp(closing[:, None] - running) * s_blocks)[:, :, None] * x_blocks
    states = jnp.einsum("kjp,kjn->kpn", weighted, b_blocks, precision=precise)
    block_rows = lax.broadcasted_iota(jnp.int32, (blocks, blocks), 0)
    block_cols = lax.broadcasted_iota(jnp.int32, (blocks, blocks), 1)
    through = jnp.dot((block_rows >= block_cols).astype(jnp.float32), closing, precision=precise)
    before = through - closing
    carry_weight = jnp.exp(
        jnp.where(block_rows > block_cols, before[:, None] - through[None, :], -1e30)
    )
    entering = (
        jnp.einsum("kj,jpn->kpn", carry_weight, states, precision=precise)
        + jnp.exp(before)[:, None, None] * start_state[None]
    )
    reading = jnp.exp(running)[:, :, None] * c_blocks
    output = output + jnp.einsum("kin,kpn->kip", reading, entering, precision=precise)
    output = output.reshape(length, head_width) + skip_gain * x_head
    final_state = (
        jnp.einsum("j,jpn->pn", jnp.exp(through[-1] - through), states, precision=precise)
        + jnp.exp(through[-1]) * start_state
    )
    return (output, final_state)


N_CHUNKS = 1


def chunk_backward(x_seq, g_seq, raw_seq, b_rows, c_rows, rate, gain):
    length = x_seq.shape[0]
    heads = raw_seq.shape[1]
    head_width = x_seq.shape[1] // heads
    runner = partial(head_forward, block_len=BLOCK)
    mapped = jax.vmap(runner, in_axes=(0, None, None, 0, 0, 0, 0))
    x_heads = x_seq.astype(jnp.float32).reshape(length, heads, head_width).transpose(1, 0, 2)
    g_heads = g_seq.astype(jnp.float32).reshape(length, heads, head_width).transpose(1, 0, 2)
    raw_heads = raw_seq.astype(jnp.float32).T
    anchor = jnp.zeros((heads, head_width, b_rows.shape[1]), jnp.float32)

    def forward(x_val, b_val, c_val, raw_val):
        return mapped(x_val, b_val, c_val, raw_val, rate, gain, anchor)[0]

    _, pullback = jax.vjp(forward, x_heads, b_rows, c_rows, raw_heads)
    grad_xh, grad_b_all, grad_c_all, grad_raw = pullback(g_heads)
    x_back = grad_xh.transpose(1, 0, 2).reshape(length, heads * head_width).astype(jnp.bfloat16)
    raw_back = grad_raw.T.astype(jnp.bfloat16)
    return x_back, raw_back, grad_b_all, grad_c_all


def gather_ctx(block, owners, me):
    if owners & (owners - 1):
        return lax.all_gather(block, "ctx", axis=0, tiled=True)
    have = block
    step = 1
    while step < owners:
        theirs = lax.ppermute(have, "ctx", [(k, k ^ step) for k in range(owners)])
        upper = (me // step) % 2 == 1
        have = jnp.where(upper, jnp.concatenate([theirs, have]), jnp.concatenate([have, theirs]))
        step *= 2
    return have


def local(x_act, b_proj, c_proj, dt_raw, a_log, d_skip, grad_out):
    rows = x_act.shape[0]
    heads_here = dt_raw.shape[1]
    head_width = x_act.shape[1] // heads_here
    state = b_proj.shape[1]
    owners = lax.axis_size("ctx")
    per_owner = heads_here // owners
    chunks = N_CHUNKS if per_owner % N_CHUNKS == 0 else 1
    per_chunk = per_owner // chunks
    me = lax.axis_index("ctx")
    half = lax.axis_index("tp")

    own_seq = lax.all_gather(jnp.where(half == 0, b_proj, c_proj), "ctx", axis=0, tiled=True)
    other_seq = lax.ppermute(own_seq, "tp", [(0, 1), (1, 0)])
    b_rows = jnp.where(half == 0, own_seq, other_seq).astype(jnp.float32)
    c_rows = jnp.where(half == 0, other_seq, own_seq).astype(jnp.float32)
    first_head = me * per_owner
    rate_own = lax.dynamic_slice_in_dim(a_log, first_head, per_owner)
    gain_own = lax.dynamic_slice_in_dim(d_skip, first_head, per_owner)

    x4 = x_act.reshape(rows, owners, per_owner, head_width)
    g4 = grad_out.reshape(rows, owners, per_owner, head_width)
    r3 = dt_raw.reshape(rows, owners, per_owner)
    x_parts, raw_parts = [], []
    grad_b_all = None
    grad_c_all = None
    for c in range(chunks):
        sl = slice(c * per_chunk, (c + 1) * per_chunk)
        width = per_chunk * head_width
        pieces = [x4[:, :, sl, :].reshape(rows, owners, width), g4[:, :, sl, :].reshape(rows, owners, width)]
        xg = jnp.concatenate(pieces, axis=2)
        xg_seq = lax.all_to_all(xg, "ctx", split_axis=1, concat_axis=0, tiled=True).reshape(rows * owners, -1)
        raw_seq = lax.all_to_all(r3[:, :, sl], "ctx", split_axis=1, concat_axis=0, tiled=True).reshape(
            rows * owners, per_chunk
        )
        x_back, raw_back, gb, gc = chunk_backward(
            xg_seq[:, :width], xg_seq[:, width : 2 * width], raw_seq, b_rows, c_rows, rate_own[sl], gain_own[sl]
        )
        x_parts.append(
            lax.all_to_all(x_back, "ctx", split_axis=0, concat_axis=1, tiled=True).reshape(rows, owners, 1, width)
        )
        raw_parts.append(
            lax.all_to_all(raw_back, "ctx", split_axis=0, concat_axis=1, tiled=True).reshape(rows, owners, 1, per_chunk)
        )
        grad_b_all = gb if grad_b_all is None else grad_b_all + gb
        grad_c_all = gc if grad_c_all is None else grad_c_all + gc
    grad_x = jnp.concatenate(x_parts, axis=2).reshape(rows, owners * per_owner * head_width)
    grad_dt = jnp.concatenate(raw_parts, axis=2).reshape(rows, heads_here)

    is_first = half == 0
    send = jnp.where(is_first, grad_c_all, grad_b_all)
    keep = jnp.where(is_first, grad_b_all, grad_c_all)
    mine = keep + lax.ppermute(send, "tp", [(0, 1), (1, 0)])
    parts = lax.all_to_all(mine.reshape(owners, rows, state), "ctx", split_axis=0, concat_axis=0, tiled=True)
    mine = parts.sum(axis=0)
    other = lax.ppermute(mine, "tp", [(0, 1), (1, 0)])
    grad_b = jnp.where(is_first, mine, other)
    grad_c = jnp.where(is_first, other, mine)
    return (grad_x, grad_b, grad_c, grad_dt)


def solution(mesh):
    in_specs = (
        P("ctx", "tp"),
        P("ctx", None),
        P("ctx", None),
        P("ctx", "tp"),
        P("tp"),
        P("tp"),
        P("ctx", "tp"),
    )
    out_specs = (P("ctx", "tp"), P("ctx", None), P("ctx", None), P("ctx", "tp"))
    return jax.shard_map(local, mesh=mesh, in_specs=in_specs, out_specs=out_specs, check_vma=False)
```

```python
from functools import partial

import jax
import jax.numpy as jnp
from jax import lax
from jax.sharding import PartitionSpec as P

BLOCK = 256


precise = lax.Precision.HIGH


def head_forward(x_head, b_rows, c_rows, raw_step, log_rate, skip_gain, start_state, block_len):
    length, head_width = x_head.shape
    blocks = length // block_len
    step_size = jax.nn.softplus(raw_step)
    decay_rates = -jnp.exp(log_rate) * step_size
    row_index = lax.broadcasted_iota(jnp.int32, (block_len, block_len), 0)
    col_index = lax.broadcasted_iota(jnp.int32, (block_len, block_len), 1)
    lower_mask = row_index >= col_index
    running = jnp.dot(
        decay_rates.reshape(blocks, block_len), lower_mask.astype(jnp.float32).T, precision=precise
    )
    between = jnp.where(lower_mask[None], running[:, :, None] - running[:, None, :], -1e30)
    x_blocks = x_head.reshape(blocks, block_len, head_width)
    b_blocks = b_rows.reshape(blocks, block_len, -1)
    c_blocks = c_rows.reshape(blocks, block_len, -1)
    s_blocks = step_size.reshape(blocks, block_len)
    scores = (
        jnp.einsum("kin,kjn->kij", c_blocks, b_blocks, precision=precise)
        * jnp.exp(between)
        * s_blocks[:, None, :]
    )
    output = jnp.einsum("kij,kjp->kip", scores, x_blocks, precision=precise)
    closing = running[:, -1]
    weighted = (jnp.exp(closing[:, None] - running) * s_blocks)[:, :, None] * x_blocks
    states = jnp.einsum("kjp,kjn->kpn", weighted, b_blocks, precision=precise)
    block_rows = lax.broadcasted_iota(jnp.int32, (blocks, blocks), 0)
    block_cols = lax.broadcasted_iota(jnp.int32, (blocks, blocks), 1)
    through = jnp.dot((block_rows >= block_cols).astype(jnp.float32), closing, precision=precise)
    before = through - closing
    carry_weight = jnp.exp(
        jnp.where(block_rows > block_cols, before[:, None] - through[None, :], -1e30)
    )
    entering = (
        jnp.einsum("kj,jpn->kpn", carry_weight, states, precision=precise)
        + jnp.exp(before)[:, None, None] * start_state[None]
    )
    reading = jnp.exp(running)[:, :, None] * c_blocks
    output = output + jnp.einsum("kin,kpn->kip", reading, entering, precision=precise)
    output = output.reshape(length, head_width) + skip_gain * x_head
    final_state = (
        jnp.einsum("j,jpn->pn", jnp.exp(through[-1] - through), states, precision=precise)
        + jnp.exp(through[-1]) * start_state
    )
    return (output, final_state)


N_CHUNKS = 1


def chunk_backward(x_seq, g_seq, raw_seq, b_rows, c_rows, rate, gain):
    length = x_seq.shape[0]
    heads = raw_seq.shape[1]
    head_width = x_seq.shape[1] // heads
    runner = partial(head_forward, block_len=BLOCK)
    mapped = jax.vmap(runner, in_axes=(0, None, None, 0, 0, 0, 0))
    x_heads = x_seq.astype(jnp.float32).reshape(length, heads, head_width).transpose(1, 0, 2)
    g_heads = g_seq.astype(jnp.float32).reshape(length, heads, head_width).transpose(1, 0, 2)
    raw_heads = raw_seq.astype(jnp.float32).T
    anchor = jnp.zeros((heads, head_width, b_rows.shape[1]), jnp.float32)

    def forward(x_val, b_val, c_val, raw_val):
        return mapped(x_val, b_val, c_val, raw_val, rate, gain, anchor)[0]

    _, pullback = jax.vjp(forward, x_heads, b_rows, c_rows, raw_heads)
    grad_xh, grad_b_all, grad_c_all, grad_raw = pullback(g_heads)
    x_back = grad_xh.transpose(1, 0, 2).reshape(length, heads * head_width).astype(jnp.bfloat16)
    raw_back = grad_raw.T.astype(jnp.bfloat16)
    return x_back, raw_back, grad_b_all, grad_c_all


def gather_ctx(block, owners, me):
    if owners & (owners - 1):
        return lax.all_gather(block, "ctx", axis=0, tiled=True)
    have = block
    step = 1
    while step < owners:
        theirs = lax.ppermute(have, "ctx", [(k, k ^ step) for k in range(owners)])
        upper = (me // step) % 2 == 1
        have = jnp.where(upper, jnp.concatenate([theirs, have]), jnp.concatenate([have, theirs]))
        step *= 2
    return have


def local(x_act, b_proj, c_proj, dt_raw, a_log, d_skip, grad_out):
    rows = x_act.shape[0]
    heads_here = dt_raw.shape[1]
    head_width = x_act.shape[1] // heads_here
    state = b_proj.shape[1]
    owners = lax.axis_size("ctx")
    per_owner = heads_here // owners
    chunks = N_CHUNKS if per_owner % N_CHUNKS == 0 else 1
    per_chunk = per_owner // chunks
    me = lax.axis_index("ctx")
    half = lax.axis_index("tp")

    own_seq = gather_ctx(jnp.where(half == 0, b_proj, c_proj), owners, me)
    other_seq = lax.ppermute(own_seq, "tp", [(0, 1), (1, 0)])
    b_rows = jnp.where(half == 0, own_seq, other_seq).astype(jnp.float32)
    c_rows = jnp.where(half == 0, other_seq, own_seq).astype(jnp.float32)
    first_head = me * per_owner
    rate_own = lax.dynamic_slice_in_dim(a_log, first_head, per_owner)
    gain_own = lax.dynamic_slice_in_dim(d_skip, first_head, per_owner)

    x4 = x_act.reshape(rows, owners, per_owner, head_width)
    g4 = grad_out.reshape(rows, owners, per_owner, head_width)
    r3 = dt_raw.reshape(rows, owners, per_owner)
    x_parts, raw_parts = [], []
    grad_b_all = None
    grad_c_all = None
    for c in range(chunks):
        sl = slice(c * per_chunk, (c + 1) * per_chunk)
        width = per_chunk * head_width
        x_seq = lax.all_to_all(
            x4[:, :, sl, :].reshape(rows, owners, width), "ctx", split_axis=1, concat_axis=0, tiled=True
        ).reshape(rows * owners, width)
        g_seq = lax.all_to_all(
            g4[:, :, sl, :].reshape(rows, owners, width), "ctx", split_axis=1, concat_axis=0, tiled=True
        ).reshape(rows * owners, width)
        raw_seq = lax.all_to_all(r3[:, :, sl], "ctx", split_axis=1, concat_axis=0, tiled=True).reshape(
            rows * owners, per_chunk
        )
        x_back, raw_back, gb, gc = chunk_backward(
            x_seq, g_seq, raw_seq, b_rows, c_rows, rate_own[sl], gain_own[sl]
        )
        x_parts.append(
            lax.all_to_all(x_back, "ctx", split_axis=0, concat_axis=1, tiled=True).reshape(rows, owners, 1, width)
        )
        raw_parts.append(
            lax.all_to_all(raw_back, "ctx", split_axis=0, concat_axis=1, tiled=True).reshape(rows, owners, 1, per_chunk)
        )
        grad_b_all = gb if grad_b_all is None else grad_b_all + gb
        grad_c_all = gc if grad_c_all is None else grad_c_all + gc
    grad_x = jnp.concatenate(x_parts, axis=2).reshape(rows, owners * per_owner * head_width)
    grad_dt = jnp.concatenate(raw_parts, axis=2).reshape(rows, heads_here)

    is_first = half == 0
    send = jnp.where(is_first, grad_c_all, grad_b_all)
    keep = jnp.where(is_first, grad_b_all, grad_c_all)
    mine = keep + lax.ppermute(send, "tp", [(0, 1), (1, 0)])
    parts = lax.all_to_all(mine.reshape(owners, rows, state), "ctx", split_axis=0, concat_axis=0, tiled=True)
    mine = parts.sum(axis=0)
    other = lax.ppermute(mine, "tp", [(0, 1), (1, 0)])
    grad_b = jnp.where(is_first, mine, other)
    grad_c = jnp.where(is_first, other, mine)
    return (grad_x, grad_b, grad_c, grad_dt)


def solution(mesh):
    in_specs = (
        P("ctx", "tp"),
        P("ctx", None),
        P("ctx", None),
        P("ctx", "tp"),
        P("tp"),
        P("tp"),
        P("ctx", "tp"),
    )
    out_specs = (P("ctx", "tp"), P("ctx", None), P("ctx", None), P("ctx", "tp"))
    return jax.shard_map(local, mesh=mesh, in_specs=in_specs, out_specs=out_specs, check_vma=False)
```

```python
from functools import partial

import jax
import jax.numpy as jnp
from jax import lax
from jax.sharding import PartitionSpec as P

BLOCK = 256


precise = lax.Precision.HIGH


def head_forward(x_head, b_rows, c_rows, raw_step, log_rate, skip_gain, start_state, block_len):
    length, head_width = x_head.shape
    blocks = length // block_len
    step_size = jax.nn.softplus(raw_step)
    decay_rates = -jnp.exp(log_rate) * step_size
    row_index = lax.broadcasted_iota(jnp.int32, (block_len, block_len), 0)
    col_index = lax.broadcasted_iota(jnp.int32, (block_len, block_len), 1)
    lower_mask = row_index >= col_index
    running = jnp.dot(
        decay_rates.reshape(blocks, block_len), lower_mask.astype(jnp.float32).T, precision=precise
    )
    between = jnp.where(lower_mask[None], running[:, :, None] - running[:, None, :], -1e30)
    x_blocks = x_head.reshape(blocks, block_len, head_width)
    b_blocks = b_rows.reshape(blocks, block_len, -1)
    c_blocks = c_rows.reshape(blocks, block_len, -1)
    s_blocks = step_size.reshape(blocks, block_len)
    scores = (
        jnp.einsum("kin,kjn->kij", c_blocks, b_blocks, precision=precise)
        * jnp.exp(between)
        * s_blocks[:, None, :]
    )
    output = jnp.einsum("kij,kjp->kip", scores, x_blocks, precision=precise)
    closing = running[:, -1]
    weighted = (jnp.exp(closing[:, None] - running) * s_blocks)[:, :, None] * x_blocks
    states = jnp.einsum("kjp,kjn->kpn", weighted, b_blocks, precision=precise)
    block_rows = lax.broadcasted_iota(jnp.int32, (blocks, blocks), 0)
    block_cols = lax.broadcasted_iota(jnp.int32, (blocks, blocks), 1)
    through = jnp.dot((block_rows >= block_cols).astype(jnp.float32), closing, precision=precise)
    before = through - closing
    carry_weight = jnp.exp(
        jnp.where(block_rows > block_cols, before[:, None] - through[None, :], -1e30)
    )
    entering = (
        jnp.einsum("kj,jpn->kpn", carry_weight, states, precision=precise)
        + jnp.exp(before)[:, None, None] * start_state[None]
    )
    reading = jnp.exp(running)[:, :, None] * c_blocks
    output = output + jnp.einsum("kin,kpn->kip", reading, entering, precision=precise)
    output = output.reshape(length, head_width) + skip_gain * x_head
    final_state = (
        jnp.einsum("j,jpn->pn", jnp.exp(through[-1] - through), states, precision=precise)
        + jnp.exp(through[-1]) * start_state
    )
    return (output, final_state)


N_CHUNKS = 1


def chunk_backward(x_seq, g_seq, raw_seq, b_rows, c_rows, rate, gain):
    length = x_seq.shape[0]
    heads = raw_seq.shape[1]
    head_width = x_seq.shape[1] // heads
    runner = partial(head_forward, block_len=BLOCK)
    mapped = jax.vmap(runner, in_axes=(0, None, None, 0, 0, 0, 0))
    x_heads = x_seq.astype(jnp.float32).reshape(length, heads, head_width).transpose(1, 0, 2)
    g_heads = g_seq.astype(jnp.float32).reshape(length, heads, head_width).transpose(1, 0, 2)
    raw_heads = raw_seq.astype(jnp.float32).T
    anchor = jnp.zeros((heads, head_width, b_rows.shape[1]), jnp.float32)

    def forward(x_val, b_val, c_val, raw_val):
        return mapped(x_val, b_val, c_val, raw_val, rate, gain, anchor)[0]

    _, pullback = jax.vjp(forward, x_heads, b_rows, c_rows, raw_heads)
    grad_xh, grad_b_all, grad_c_all, grad_raw = pullback(g_heads)
    x_back = grad_xh.transpose(1, 0, 2).reshape(length, heads * head_width).astype(jnp.bfloat16)
    raw_back = grad_raw.T.astype(jnp.bfloat16)
    return x_back, raw_back, grad_b_all, grad_c_all


def gather_ctx(block, owners, me):
    if owners & (owners - 1):
        return lax.all_gather(block, "ctx", axis=0, tiled=True)
    have = block
    step = 1
    while step < owners:
        theirs = lax.ppermute(have, "ctx", [(k, k ^ step) for k in range(owners)])
        upper = (me // step) % 2 == 1
        have = jnp.where(upper, jnp.concatenate([theirs, have]), jnp.concatenate([have, theirs]))
        step *= 2
    return have


def local(x_act, b_proj, c_proj, dt_raw, a_log, d_skip, grad_out):
    rows = x_act.shape[0]
    heads_here = dt_raw.shape[1]
    head_width = x_act.shape[1] // heads_here
    state = b_proj.shape[1]
    owners = lax.axis_size("ctx")
    per_owner = heads_here // owners
    chunks = N_CHUNKS if per_owner % N_CHUNKS == 0 else 1
    per_chunk = per_owner // chunks
    me = lax.axis_index("ctx")
    half = lax.axis_index("tp")

    own_seq = gather_ctx(jnp.where(half == 0, b_proj, c_proj), owners, me)
    other_seq = lax.ppermute(own_seq, "tp", [(0, 1), (1, 0)])
    b_rows = jnp.where(half == 0, own_seq, other_seq).astype(jnp.float32)
    c_rows = jnp.where(half == 0, other_seq, own_seq).astype(jnp.float32)
    first_head = me * per_owner
    rate_own = lax.dynamic_slice_in_dim(a_log, first_head, per_owner)
    gain_own = lax.dynamic_slice_in_dim(d_skip, first_head, per_owner)

    x4 = x_act.reshape(rows, owners, per_owner, head_width)
    g4 = grad_out.reshape(rows, owners, per_owner, head_width)
    r3 = dt_raw.reshape(rows, owners, per_owner)
    x_parts, raw_parts = [], []
    grad_b_all = None
    grad_c_all = None
    for c in range(chunks):
        sl = slice(c * per_chunk, (c + 1) * per_chunk)
        width = per_chunk * head_width
        x_in = x4[:, :, sl, :].reshape(rows, owners, width)
        g_in = g4[:, :, sl, :].reshape(rows, owners, width)
        if c == 0:
            x_in, g_in, _ = lax.optimization_barrier((x_in, g_in, own_seq))
        x_seq = lax.all_to_all(x_in, "ctx", split_axis=1, concat_axis=0, tiled=True).reshape(rows * owners, width)
        g_seq = lax.all_to_all(g_in, "ctx", split_axis=1, concat_axis=0, tiled=True).reshape(rows * owners, width)
        raw_seq = lax.all_to_all(r3[:, :, sl], "ctx", split_axis=1, concat_axis=0, tiled=True).reshape(
            rows * owners, per_chunk
        )
        x_back, raw_back, gb, gc = chunk_backward(
            x_seq, g_seq, raw_seq, b_rows, c_rows, rate_own[sl], gain_own[sl]
        )
        x_parts.append(
            lax.all_to_all(x_back, "ctx", split_axis=0, concat_axis=1, tiled=True).reshape(rows, owners, 1, width)
        )
        raw_parts.append(
            lax.all_to_all(raw_back, "ctx", split_axis=0, concat_axis=1, tiled=True).reshape(rows, owners, 1, per_chunk)
        )
        grad_b_all = gb if grad_b_all is None else grad_b_all + gb
        grad_c_all = gc if grad_c_all is None else grad_c_all + gc
    grad_x = jnp.concatenate(x_parts, axis=2).reshape(rows, owners * per_owner * head_width)
    grad_dt = jnp.concatenate(raw_parts, axis=2).reshape(rows, heads_here)

    is_first = half == 0
    send = jnp.where(is_first, grad_c_all, grad_b_all)
    keep = jnp.where(is_first, grad_b_all, grad_c_all)
    mine = keep + lax.ppermute(send, "tp", [(0, 1), (1, 0)])
    parts = lax.all_to_all(mine.reshape(owners, rows, state), "ctx", split_axis=0, concat_axis=0, tiled=True)
    mine = parts.sum(axis=0)
    other = lax.ppermute(mine, "tp", [(0, 1), (1, 0)])
    grad_b = jnp.where(is_first, mine, other)
    grad_c = jnp.where(is_first, other, mine)
    return (grad_x, grad_b, grad_c, grad_dt)


def solution(mesh):
    in_specs = (
        P("ctx", "tp"),
        P("ctx", None),
        P("ctx", None),
        P("ctx", "tp"),
        P("tp"),
        P("tp"),
        P("ctx", "tp"),
    )
    out_specs = (P("ctx", "tp"), P("ctx", None), P("ctx", None), P("ctx", "tp"))
    return jax.shard_map(local, mesh=mesh, in_specs=in_specs, out_specs=out_specs, check_vma=False)
```

```python
from functools import partial

import jax
import jax.numpy as jnp
from jax import lax
from jax.sharding import PartitionSpec as P

BLOCK = 256


precise = lax.Precision.HIGH


def head_forward(x_head, b_rows, c_rows, raw_step, log_rate, skip_gain, start_state, block_len):
    length, head_width = x_head.shape
    blocks = length // block_len
    step_size = jax.nn.softplus(raw_step)
    decay_rates = -jnp.exp(log_rate) * step_size
    row_index = lax.broadcasted_iota(jnp.int32, (block_len, block_len), 0)
    col_index = lax.broadcasted_iota(jnp.int32, (block_len, block_len), 1)
    lower_mask = row_index >= col_index
    running = jnp.dot(
        decay_rates.reshape(blocks, block_len), lower_mask.astype(jnp.float32).T, precision=precise
    )
    between = jnp.where(lower_mask[None], running[:, :, None] - running[:, None, :], -1e30)
    x_blocks = x_head.reshape(blocks, block_len, head_width)
    b_blocks = b_rows.reshape(blocks, block_len, -1)
    c_blocks = c_rows.reshape(blocks, block_len, -1)
    s_blocks = step_size.reshape(blocks, block_len)
    scores = (
        jnp.einsum("kin,kjn->kij", c_blocks, b_blocks, precision=precise)
        * jnp.exp(between)
        * s_blocks[:, None, :]
    )
    output = jnp.einsum("kij,kjp->kip", scores, x_blocks, precision=precise)
    closing = running[:, -1]
    weighted = (jnp.exp(closing[:, None] - running) * s_blocks)[:, :, None] * x_blocks
    states = jnp.einsum("kjp,kjn->kpn", weighted, b_blocks, precision=precise)
    block_rows = lax.broadcasted_iota(jnp.int32, (blocks, blocks), 0)
    block_cols = lax.broadcasted_iota(jnp.int32, (blocks, blocks), 1)
    through = jnp.dot((block_rows >= block_cols).astype(jnp.float32), closing, precision=precise)
    before = through - closing
    carry_weight = jnp.exp(
        jnp.where(block_rows > block_cols, before[:, None] - through[None, :], -1e30)
    )
    entering = (
        jnp.einsum("kj,jpn->kpn", carry_weight, states, precision=precise)
        + jnp.exp(before)[:, None, None] * start_state[None]
    )
    reading = jnp.exp(running)[:, :, None] * c_blocks
    output = output + jnp.einsum("kin,kpn->kip", reading, entering, precision=precise)
    output = output.reshape(length, head_width) + skip_gain * x_head
    final_state = (
        jnp.einsum("j,jpn->pn", jnp.exp(through[-1] - through), states, precision=precise)
        + jnp.exp(through[-1]) * start_state
    )
    return (output, final_state)


N_CHUNKS = 1


def chunk_backward(x_seq, g_seq, raw_seq, b_rows, c_rows, rate, gain):
    length = x_seq.shape[0]
    heads = raw_seq.shape[1]
    head_width = x_seq.shape[1] // heads
    runner = partial(head_forward, block_len=BLOCK)
    mapped = jax.vmap(runner, in_axes=(0, None, None, 0, 0, 0, 0))
    x_heads = x_seq.astype(jnp.float32).reshape(length, heads, head_width).transpose(1, 0, 2)
    g_heads = g_seq.astype(jnp.float32).reshape(length, heads, head_width).transpose(1, 0, 2)
    raw_heads = raw_seq.astype(jnp.float32).T
    anchor = jnp.zeros((heads, head_width, b_rows.shape[1]), jnp.float32)

    def forward(x_val, b_val, c_val, raw_val):
        return mapped(x_val, b_val, c_val, raw_val, rate, gain, anchor)[0]

    _, pullback = jax.vjp(forward, x_heads, b_rows, c_rows, raw_heads)
    grad_xh, grad_b_all, grad_c_all, grad_raw = pullback(g_heads)
    x_back = grad_xh.transpose(1, 0, 2).reshape(length, heads * head_width).astype(jnp.bfloat16)
    raw_back = grad_raw.T.astype(jnp.bfloat16)
    return x_back, raw_back, grad_b_all, grad_c_all


def gather_ctx(block, owners, me):
    if owners & (owners - 1):
        return lax.all_gather(block, "ctx", axis=0, tiled=True)
    have = block
    step = 1
    while step < owners:
        theirs = lax.ppermute(have, "ctx", [(k, k ^ step) for k in range(owners)])
        upper = (me // step) % 2 == 1
        have = jnp.where(upper, jnp.concatenate([theirs, have]), jnp.concatenate([have, theirs]))
        step *= 2
    return have


def local(x_act, b_proj, c_proj, dt_raw, a_log, d_skip, grad_out):
    rows = x_act.shape[0]
    heads_here = dt_raw.shape[1]
    head_width = x_act.shape[1] // heads_here
    state = b_proj.shape[1]
    owners = lax.axis_size("ctx")
    per_owner = heads_here // owners
    chunks = N_CHUNKS if per_owner % N_CHUNKS == 0 else 1
    per_chunk = per_owner // chunks
    me = lax.axis_index("ctx")
    half = lax.axis_index("tp")

    own_seq = gather_ctx(jnp.where(half == 0, b_proj, c_proj), owners, me)
    other_seq = lax.ppermute(own_seq, "tp", [(0, 1), (1, 0)])
    b_rows = jnp.where(half == 0, own_seq, other_seq).astype(jnp.float32)
    c_rows = jnp.where(half == 0, other_seq, own_seq).astype(jnp.float32)
    first_head = me * per_owner
    rate_own = lax.dynamic_slice_in_dim(a_log, first_head, per_owner)
    gain_own = lax.dynamic_slice_in_dim(d_skip, first_head, per_owner)

    x4 = x_act.reshape(rows, owners, per_owner, head_width)
    g4 = grad_out.reshape(rows, owners, per_owner, head_width)
    r3 = dt_raw.reshape(rows, owners, per_owner)
    x_parts, raw_parts = [], []
    grad_b_all = None
    grad_c_all = None
    for c in range(chunks):
        sl = slice(c * per_chunk, (c + 1) * per_chunk)
        width = per_chunk * head_width
        x_in = x4[:, :, sl, :].reshape(rows, owners, width)
        g_in = g4[:, :, sl, :].reshape(rows, owners, width)
        if c == 0:
            x_in, g_in, _ = lax.optimization_barrier((x_in, g_in, own_seq))
        x_seq = lax.all_to_all(x_in, "ctx", split_axis=1, concat_axis=0, tiled=True).reshape(rows * owners, width)
        g_seq = lax.all_to_all(g_in, "ctx", split_axis=1, concat_axis=0, tiled=True).reshape(rows * owners, width)
        raw_seq = lax.all_to_all(r3[:, :, sl], "ctx", split_axis=1, concat_axis=0, tiled=True).reshape(
            rows * owners, per_chunk
        )
        x_back, raw_back, gb, gc = chunk_backward(
            x_seq, g_seq, raw_seq, b_rows, c_rows, rate_own[sl], gain_own[sl]
        )
        back = x_back.reshape(owners, rows, width)
        steps_back = raw_back.reshape(owners, rows, per_chunk).transpose(0, 2, 1)
        extra = (per_chunk * rows) // width
        if extra * width == per_chunk * rows:
            packed = jnp.concatenate([back, steps_back.reshape(owners, extra, width)], axis=1)
            got = lax.all_to_all(packed, "ctx", split_axis=0, concat_axis=0, tiled=True)
            got_x = got[:, :rows, :]
            got_dt = got[:, rows:, :].reshape(owners, per_chunk, rows)
        else:
            got_x = lax.all_to_all(back, "ctx", split_axis=0, concat_axis=0, tiled=True)
            got_dt = lax.all_to_all(steps_back, "ctx", split_axis=0, concat_axis=0, tiled=True)
        x_parts.append(got_x.transpose(1, 0, 2).reshape(rows, owners, 1, width))
        raw_parts.append(got_dt.transpose(2, 0, 1).reshape(rows, owners, 1, per_chunk))
        grad_b_all = gb if grad_b_all is None else grad_b_all + gb
        grad_c_all = gc if grad_c_all is None else grad_c_all + gc
    grad_x = jnp.concatenate(x_parts, axis=2).reshape(rows, owners * per_owner * head_width)
    grad_dt = jnp.concatenate(raw_parts, axis=2).reshape(rows, heads_here)

    is_first = half == 0
    send = jnp.where(is_first, grad_c_all, grad_b_all)
    keep = jnp.where(is_first, grad_b_all, grad_c_all)
    mine = keep + lax.ppermute(send, "tp", [(0, 1), (1, 0)])
    parts = lax.all_to_all(mine.reshape(owners, rows, state), "ctx", split_axis=0, concat_axis=0, tiled=True)
    mine = parts.sum(axis=0)
    other = lax.ppermute(mine, "tp", [(0, 1), (1, 0)])
    grad_b = jnp.where(is_first, mine, other)
    grad_c = jnp.where(is_first, other, mine)
    return (grad_x, grad_b, grad_c, grad_dt)


def solution(mesh):
    in_specs = (
        P("ctx", "tp"),
        P("ctx", None),
        P("ctx", None),
        P("ctx", "tp"),
        P("tp"),
        P("tp"),
        P("ctx", "tp"),
    )
    out_specs = (P("ctx", "tp"), P("ctx", None), P("ctx", None), P("ctx", "tp"))
    return jax.shard_map(local, mesh=mesh, in_specs=in_specs, out_specs=out_specs, check_vma=False)
```

```python
from functools import partial

import jax
import jax.numpy as jnp
from jax import lax
from jax.sharding import PartitionSpec as P

BLOCK = 256


precise = lax.Precision.HIGH


def head_forward(x_head, b_rows, c_rows, raw_step, log_rate, skip_gain, start_state, block_len):
    length, head_width = x_head.shape
    blocks = length // block_len
    step_size = jax.nn.softplus(raw_step)
    decay_rates = -jnp.exp(log_rate) * step_size
    row_index = lax.broadcasted_iota(jnp.int32, (block_len, block_len), 0)
    col_index = lax.broadcasted_iota(jnp.int32, (block_len, block_len), 1)
    lower_mask = row_index >= col_index
    running = jnp.dot(
        decay_rates.reshape(blocks, block_len), lower_mask.astype(jnp.float32).T, precision=precise
    )
    between = jnp.where(lower_mask[None], running[:, :, None] - running[:, None, :], -1e30)
    x_blocks = x_head.reshape(blocks, block_len, head_width)
    b_blocks = b_rows.reshape(blocks, block_len, -1)
    c_blocks = c_rows.reshape(blocks, block_len, -1)
    s_blocks = step_size.reshape(blocks, block_len)
    scores = (
        jnp.einsum("kin,kjn->kij", c_blocks, b_blocks, precision=precise)
        * jnp.exp(between)
        * s_blocks[:, None, :]
    )
    output = jnp.einsum("kij,kjp->kip", scores, x_blocks, precision=precise)
    closing = running[:, -1]
    weighted = (jnp.exp(closing[:, None] - running) * s_blocks)[:, :, None] * x_blocks
    states = jnp.einsum("kjp,kjn->kpn", weighted, b_blocks, precision=precise)
    block_rows = lax.broadcasted_iota(jnp.int32, (blocks, blocks), 0)
    block_cols = lax.broadcasted_iota(jnp.int32, (blocks, blocks), 1)
    through = jnp.dot((block_rows >= block_cols).astype(jnp.float32), closing, precision=precise)
    before = through - closing
    carry_weight = jnp.exp(
        jnp.where(block_rows > block_cols, before[:, None] - through[None, :], -1e30)
    )
    entering = (
        jnp.einsum("kj,jpn->kpn", carry_weight, states, precision=precise)
        + jnp.exp(before)[:, None, None] * start_state[None]
    )
    reading = jnp.exp(running)[:, :, None] * c_blocks
    output = output + jnp.einsum("kin,kpn->kip", reading, entering, precision=precise)
    output = output.reshape(length, head_width) + skip_gain * x_head
    final_state = (
        jnp.einsum("j,jpn->pn", jnp.exp(through[-1] - through), states, precision=precise)
        + jnp.exp(through[-1]) * start_state
    )
    return (output, final_state)


N_CHUNKS = 1


def chunk_backward(x_seq, g_seq, raw_seq, b_rows, c_rows, rate, gain):
    length = x_seq.shape[0]
    heads = raw_seq.shape[1]
    head_width = x_seq.shape[1] // heads
    runner = partial(head_forward, block_len=BLOCK)
    mapped = jax.vmap(runner, in_axes=(0, None, None, 0, 0, 0, 0))
    x_heads = x_seq.astype(jnp.float32).reshape(length, heads, head_width).transpose(1, 0, 2)
    g_heads = g_seq.astype(jnp.float32).reshape(length, heads, head_width).transpose(1, 0, 2)
    raw_heads = raw_seq.astype(jnp.float32).T
    anchor = jnp.zeros((heads, head_width, b_rows.shape[1]), jnp.float32)

    def forward(x_val, b_val, c_val, raw_val):
        return mapped(x_val, b_val, c_val, raw_val, rate, gain, anchor)[0]

    _, pullback = jax.vjp(forward, x_heads, b_rows, c_rows, raw_heads)
    grad_xh, grad_b_all, grad_c_all, grad_raw = pullback(g_heads)
    x_back = grad_xh.transpose(1, 0, 2).reshape(length, heads * head_width).astype(jnp.bfloat16)
    raw_back = grad_raw.T.astype(jnp.bfloat16)
    return x_back, raw_back, grad_b_all, grad_c_all


def gather_ctx(block, owners, me):
    if owners & (owners - 1):
        return lax.all_gather(block, "ctx", axis=0, tiled=True)
    have = block
    step = 1
    while step < owners:
        theirs = lax.ppermute(have, "ctx", [(k, k ^ step) for k in range(owners)])
        upper = (me // step) % 2 == 1
        have = jnp.where(upper, jnp.concatenate([theirs, have]), jnp.concatenate([have, theirs]))
        step *= 2
    return have


def local(x_act, b_proj, c_proj, dt_raw, a_log, d_skip, grad_out):
    rows = x_act.shape[0]
    heads_here = dt_raw.shape[1]
    head_width = x_act.shape[1] // heads_here
    state = b_proj.shape[1]
    owners = lax.axis_size("ctx")
    per_owner = heads_here // owners
    chunks = N_CHUNKS if per_owner % N_CHUNKS == 0 else 1
    per_chunk = per_owner // chunks
    me = lax.axis_index("ctx")
    half = lax.axis_index("tp")

    own_seq = gather_ctx(jnp.where(half == 0, b_proj, c_proj), owners, me)
    other_seq = lax.ppermute(own_seq, "tp", [(0, 1), (1, 0)])
    b_rows = jnp.where(half == 0, own_seq, other_seq).astype(jnp.float32)
    c_rows = jnp.where(half == 0, other_seq, own_seq).astype(jnp.float32)
    first_head = me * per_owner
    rate_own = lax.dynamic_slice_in_dim(a_log, first_head, per_owner)
    gain_own = lax.dynamic_slice_in_dim(d_skip, first_head, per_owner)

    x4 = x_act.reshape(rows, owners, per_owner, head_width)
    g4 = grad_out.reshape(rows, owners, per_owner, head_width)
    r3 = dt_raw.reshape(rows, owners, per_owner)
    x_parts, raw_parts = [], []
    grad_b_all = None
    grad_c_all = None
    for c in range(chunks):
        sl = slice(c * per_chunk, (c + 1) * per_chunk)
        width = per_chunk * head_width
        x_in = x4[:, :, sl, :].reshape(rows, owners, width)
        g_in = g4[:, :, sl, :].reshape(rows, owners, width)
        if c == 0:
            g_in, _ = lax.optimization_barrier((g_in, own_seq))
        x_seq = lax.all_to_all(x_in, "ctx", split_axis=1, concat_axis=0, tiled=True).reshape(rows * owners, width)
        g_seq = lax.all_to_all(g_in, "ctx", split_axis=1, concat_axis=0, tiled=True).reshape(rows * owners, width)
        raw_seq = lax.all_to_all(r3[:, :, sl], "ctx", split_axis=1, concat_axis=0, tiled=True).reshape(
            rows * owners, per_chunk
        )
        x_back, raw_back, gb, gc = chunk_backward(
            x_seq, g_seq, raw_seq, b_rows, c_rows, rate_own[sl], gain_own[sl]
        )
        x_parts.append(
            lax.all_to_all(x_back, "ctx", split_axis=0, concat_axis=1, tiled=True).reshape(rows, owners, 1, width)
        )
        raw_parts.append(
            lax.all_to_all(raw_back, "ctx", split_axis=0, concat_axis=1, tiled=True).reshape(rows, owners, 1, per_chunk)
        )
        grad_b_all = gb if grad_b_all is None else grad_b_all + gb
        grad_c_all = gc if grad_c_all is None else grad_c_all + gc
    grad_x = jnp.concatenate(x_parts, axis=2).reshape(rows, owners * per_owner * head_width)
    grad_dt = jnp.concatenate(raw_parts, axis=2).reshape(rows, heads_here)

    is_first = half == 0
    send = jnp.where(is_first, grad_c_all, grad_b_all)
    keep = jnp.where(is_first, grad_b_all, grad_c_all)
    mine = keep + lax.ppermute(send, "tp", [(0, 1), (1, 0)])
    parts = lax.all_to_all(mine.reshape(owners, rows, state), "ctx", split_axis=0, concat_axis=0, tiled=True)
    mine = parts.sum(axis=0)
    other = lax.ppermute(mine, "tp", [(0, 1), (1, 0)])
    grad_b = jnp.where(is_first, mine, other)
    grad_c = jnp.where(is_first, other, mine)
    return (grad_x, grad_b, grad_c, grad_dt)


def solution(mesh):
    in_specs = (
        P("ctx", "tp"),
        P("ctx", None),
        P("ctx", None),
        P("ctx", "tp"),
        P("tp"),
        P("tp"),
        P("ctx", "tp"),
    )
    out_specs = (P("ctx", "tp"), P("ctx", None), P("ctx", None), P("ctx", "tp"))
    return jax.shard_map(local, mesh=mesh, in_specs=in_specs, out_specs=out_specs, check_vma=False)
```

```python
from functools import partial

import jax
import jax.numpy as jnp
from jax import lax
from jax.sharding import PartitionSpec as P

BLOCK = 256


precise = lax.Precision.HIGH


def head_forward(x_head, b_rows, c_rows, raw_step, log_rate, skip_gain, start_state, block_len):
    length, head_width = x_head.shape
    blocks = length // block_len
    step_size = jax.nn.softplus(raw_step)
    decay_rates = -jnp.exp(log_rate) * step_size
    row_index = lax.broadcasted_iota(jnp.int32, (block_len, block_len), 0)
    col_index = lax.broadcasted_iota(jnp.int32, (block_len, block_len), 1)
    lower_mask = row_index >= col_index
    running = jnp.dot(
        decay_rates.reshape(blocks, block_len), lower_mask.astype(jnp.float32).T, precision=precise
    )
    between = jnp.where(lower_mask[None], running[:, :, None] - running[:, None, :], -1e30)
    x_blocks = x_head.reshape(blocks, block_len, head_width)
    b_blocks = b_rows.reshape(blocks, block_len, -1)
    c_blocks = c_rows.reshape(blocks, block_len, -1)
    s_blocks = step_size.reshape(blocks, block_len)
    scores = (
        jnp.einsum("kin,kjn->kij", c_blocks, b_blocks, precision=precise)
        * jnp.exp(between)
        * s_blocks[:, None, :]
    )
    output = jnp.einsum("kij,kjp->kip", scores, x_blocks, precision=precise)
    closing = running[:, -1]
    weighted = (jnp.exp(closing[:, None] - running) * s_blocks)[:, :, None] * x_blocks
    states = jnp.einsum("kjp,kjn->kpn", weighted, b_blocks, precision=precise)
    block_rows = lax.broadcasted_iota(jnp.int32, (blocks, blocks), 0)
    block_cols = lax.broadcasted_iota(jnp.int32, (blocks, blocks), 1)
    through = jnp.dot((block_rows >= block_cols).astype(jnp.float32), closing, precision=precise)
    before = through - closing
    carry_weight = jnp.exp(
        jnp.where(block_rows > block_cols, before[:, None] - through[None, :], -1e30)
    )
    entering = (
        jnp.einsum("kj,jpn->kpn", carry_weight, states, precision=precise)
        + jnp.exp(before)[:, None, None] * start_state[None]
    )
    reading = jnp.exp(running)[:, :, None] * c_blocks
    output = output + jnp.einsum("kin,kpn->kip", reading, entering, precision=precise)
    output = output.reshape(length, head_width) + skip_gain * x_head
    final_state = (
        jnp.einsum("j,jpn->pn", jnp.exp(through[-1] - through), states, precision=precise)
        + jnp.exp(through[-1]) * start_state
    )
    return (output, final_state)


N_CHUNKS = 1


def chunk_backward(x_seq, g_seq, raw_seq, b_rows, c_rows, rate, gain):
    length = x_seq.shape[0]
    heads = raw_seq.shape[1]
    head_width = x_seq.shape[1] // heads
    runner = partial(head_forward, block_len=BLOCK)
    mapped = jax.vmap(runner, in_axes=(0, None, None, 0, 0, 0, 0))
    x_heads = x_seq.astype(jnp.float32).reshape(length, heads, head_width).transpose(1, 0, 2)
    g_heads = g_seq.astype(jnp.float32).reshape(length, heads, head_width).transpose(1, 0, 2)
    raw_heads = raw_seq.astype(jnp.float32).T
    anchor = jnp.zeros((heads, head_width, b_rows.shape[1]), jnp.float32)

    def forward(x_val, b_val, c_val, raw_val):
        return mapped(x_val, b_val, c_val, raw_val, rate, gain, anchor)[0]

    _, pullback = jax.vjp(forward, x_heads, b_rows, c_rows, raw_heads)
    grad_xh, grad_b_all, grad_c_all, grad_raw = pullback(g_heads)
    x_back = grad_xh.transpose(1, 0, 2).reshape(length, heads * head_width).astype(jnp.bfloat16)
    raw_back = grad_raw.T.astype(jnp.bfloat16)
    return x_back, raw_back, grad_b_all, grad_c_all


def gather_ctx(block, owners, me):
    if owners & (owners - 1):
        return lax.all_gather(block, "ctx", axis=0, tiled=True)
    have = block
    step = 1
    while step < owners:
        theirs = lax.ppermute(have, "ctx", [(k, k ^ step) for k in range(owners)])
        upper = (me // step) % 2 == 1
        have = jnp.where(upper, jnp.concatenate([theirs, have]), jnp.concatenate([have, theirs]))
        step *= 2
    return have


def local(x_act, b_proj, c_proj, dt_raw, a_log, d_skip, grad_out):
    rows = x_act.shape[0]
    heads_here = dt_raw.shape[1]
    head_width = x_act.shape[1] // heads_here
    state = b_proj.shape[1]
    owners = lax.axis_size("ctx")
    per_owner = heads_here // owners
    chunks = N_CHUNKS if per_owner % N_CHUNKS == 0 else 1
    per_chunk = per_owner // chunks
    me = lax.axis_index("ctx")
    half = lax.axis_index("tp")

    own_seq = gather_ctx(jnp.where(half == 0, b_proj, c_proj), owners, me)
    other_seq = lax.ppermute(own_seq, "tp", [(0, 1), (1, 0)])
    b_rows = jnp.where(half == 0, own_seq, other_seq).astype(jnp.float32)
    c_rows = jnp.where(half == 0, other_seq, own_seq).astype(jnp.float32)
    first_head = me * per_owner
    rate_own = lax.dynamic_slice_in_dim(a_log, first_head, per_owner)
    gain_own = lax.dynamic_slice_in_dim(d_skip, first_head, per_owner)

    x4 = x_act.reshape(rows, owners, per_owner, head_width)
    g4 = grad_out.reshape(rows, owners, per_owner, head_width)
    r3 = dt_raw.reshape(rows, owners, per_owner)
    x_parts, raw_parts = [], []
    grad_b_all = None
    grad_c_all = None
    for c in range(chunks):
        sl = slice(c * per_chunk, (c + 1) * per_chunk)
        width = per_chunk * head_width
        x_in = x4[:, :, sl, :].reshape(rows, owners, width)
        g_in = g4[:, :, sl, :].reshape(rows, owners, width)
        if c == 0:
            g_in, _ = lax.optimization_barrier((g_in, own_seq))
        x_seq = lax.all_to_all(x_in, "ctx", split_axis=1, concat_axis=0, tiled=True).reshape(rows * owners, width)
        g_seq = lax.all_to_all(g_in, "ctx", split_axis=1, concat_axis=0, tiled=True).reshape(rows * owners, width)
        raw_seq = lax.all_to_all(r3[:, :, sl], "ctx", split_axis=1, concat_axis=0, tiled=True).reshape(
            rows * owners, per_chunk
        )
        x_back, raw_back, gb, gc = chunk_backward(
            x_seq, g_seq, raw_seq, b_rows, c_rows, rate_own[sl], gain_own[sl]
        )
        x_parts.append(
            lax.all_to_all(x_back, "ctx", split_axis=0, concat_axis=1, tiled=True).reshape(rows, owners, 1, width)
        )
        raw_parts.append(
            lax.all_to_all(raw_back, "ctx", split_axis=0, concat_axis=1, tiled=True).reshape(rows, owners, 1, per_chunk)
        )
        grad_b_all = gb if grad_b_all is None else grad_b_all + gb
        grad_c_all = gc if grad_c_all is None else grad_c_all + gc
    grad_x = jnp.concatenate(x_parts, axis=2).reshape(rows, owners * per_owner * head_width)
    grad_dt = jnp.concatenate(raw_parts, axis=2).reshape(rows, heads_here)

    is_first = half == 0
    send = jnp.where(is_first, grad_c_all, grad_b_all)
    keep = jnp.where(is_first, grad_b_all, grad_c_all)
    mine = keep + lax.ppermute(send, "tp", [(0, 1), (1, 0)])
    mine = lax.psum_scatter(mine, "ctx", scatter_dimension=0, tiled=True)
    other = lax.ppermute(mine, "tp", [(0, 1), (1, 0)])
    grad_b = jnp.where(is_first, mine, other)
    grad_c = jnp.where(is_first, other, mine)
    return (grad_x, grad_b, grad_c, grad_dt)


def solution(mesh):
    in_specs = (
        P("ctx", "tp"),
        P("ctx", None),
        P("ctx", None),
        P("ctx", "tp"),
        P("tp"),
        P("tp"),
        P("ctx", "tp"),
    )
    out_specs = (P("ctx", "tp"), P("ctx", None), P("ctx", None), P("ctx", "tp"))
    return jax.shard_map(local, mesh=mesh, in_specs=in_specs, out_specs=out_specs, check_vma=False)
```

```python
from functools import partial

import jax
import jax.numpy as jnp
from jax import lax
from jax.sharding import PartitionSpec as P

BLOCK = 256


precise = lax.Precision.HIGH


def head_forward(x_head, b_rows, c_rows, raw_step, log_rate, skip_gain, start_state, block_len):
    length, head_width = x_head.shape
    blocks = length // block_len
    step_size = jax.nn.softplus(raw_step)
    decay_rates = -jnp.exp(log_rate) * step_size
    row_index = lax.broadcasted_iota(jnp.int32, (block_len, block_len), 0)
    col_index = lax.broadcasted_iota(jnp.int32, (block_len, block_len), 1)
    lower_mask = row_index >= col_index
    running = jnp.dot(
        decay_rates.reshape(blocks, block_len), lower_mask.astype(jnp.float32).T, precision=precise
    )
    between = jnp.where(lower_mask[None], running[:, :, None] - running[:, None, :], -1e30)
    x_blocks = x_head.reshape(blocks, block_len, head_width)
    b_blocks = b_rows.reshape(blocks, block_len, -1)
    c_blocks = c_rows.reshape(blocks, block_len, -1)
    s_blocks = step_size.reshape(blocks, block_len)
    scores = (
        jnp.einsum("kin,kjn->kij", c_blocks, b_blocks, precision=precise)
        * jnp.exp(between)
        * s_blocks[:, None, :]
    )
    output = jnp.einsum("kij,kjp->kip", scores, x_blocks, precision=precise)
    closing = running[:, -1]
    weighted = (jnp.exp(closing[:, None] - running) * s_blocks)[:, :, None] * x_blocks
    states = jnp.einsum("kjp,kjn->kpn", weighted, b_blocks, precision=precise)
    block_rows = lax.broadcasted_iota(jnp.int32, (blocks, blocks), 0)
    block_cols = lax.broadcasted_iota(jnp.int32, (blocks, blocks), 1)
    through = jnp.dot((block_rows >= block_cols).astype(jnp.float32), closing, precision=precise)
    before = through - closing
    carry_weight = jnp.exp(
        jnp.where(block_rows > block_cols, before[:, None] - through[None, :], -1e30)
    )
    entering = (
        jnp.einsum("kj,jpn->kpn", carry_weight, states, precision=precise)
        + jnp.exp(before)[:, None, None] * start_state[None]
    )
    reading = jnp.exp(running)[:, :, None] * c_blocks
    output = output + jnp.einsum("kin,kpn->kip", reading, entering, precision=precise)
    output = output.reshape(length, head_width) + skip_gain * x_head
    final_state = (
        jnp.einsum("j,jpn->pn", jnp.exp(through[-1] - through), states, precision=precise)
        + jnp.exp(through[-1]) * start_state
    )
    return (output, final_state)


N_CHUNKS = 1


def chunk_backward(x_seq, g_seq, raw_seq, b_rows, c_rows, rate, gain):
    length = x_seq.shape[0]
    heads = raw_seq.shape[1]
    head_width = x_seq.shape[1] // heads
    runner = partial(head_forward, block_len=BLOCK)
    mapped = jax.vmap(runner, in_axes=(0, None, None, 0, 0, 0, 0))
    x_heads = x_seq.astype(jnp.float32).reshape(length, heads, head_width).transpose(1, 0, 2)
    g_heads = g_seq.astype(jnp.float32).reshape(length, heads, head_width).transpose(1, 0, 2)
    raw_heads = raw_seq.astype(jnp.float32).T
    anchor = jnp.zeros((heads, head_width, b_rows.shape[1]), jnp.float32)

    def forward(x_val, b_val, c_val, raw_val):
        return mapped(x_val, b_val, c_val, raw_val, rate, gain, anchor)[0]

    _, pullback = jax.vjp(forward, x_heads, b_rows, c_rows, raw_heads)
    grad_xh, grad_b_all, grad_c_all, grad_raw = pullback(g_heads)
    x_back = grad_xh.transpose(1, 0, 2).reshape(length, heads * head_width).astype(jnp.bfloat16)
    raw_back = grad_raw.T
    return x_back, raw_back, grad_b_all, grad_c_all


def gather_ctx(block, owners, me):
    if owners & (owners - 1):
        return lax.all_gather(block, "ctx", axis=0, tiled=True)
    have = block
    step = 1
    while step < owners:
        theirs = lax.ppermute(have, "ctx", [(k, k ^ step) for k in range(owners)])
        upper = (me // step) % 2 == 1
        have = jnp.where(upper, jnp.concatenate([theirs, have]), jnp.concatenate([have, theirs]))
        step *= 2
    return have


def local(x_act, b_proj, c_proj, dt_raw, a_log, d_skip, grad_out):
    rows = x_act.shape[0]
    heads_here = dt_raw.shape[1]
    head_width = x_act.shape[1] // heads_here
    state = b_proj.shape[1]
    owners = lax.axis_size("ctx")
    per_owner = heads_here // owners
    chunks = N_CHUNKS if per_owner % N_CHUNKS == 0 else 1
    per_chunk = per_owner // chunks
    me = lax.axis_index("ctx")
    half = lax.axis_index("tp")

    own_seq = gather_ctx(jnp.where(half == 0, b_proj, c_proj), owners, me)
    other_seq = lax.ppermute(own_seq, "tp", [(0, 1), (1, 0)])
    b_rows = jnp.where(half == 0, own_seq, other_seq).astype(jnp.float32)
    c_rows = jnp.where(half == 0, other_seq, own_seq).astype(jnp.float32)
    first_head = me * per_owner
    rate_own = lax.dynamic_slice_in_dim(a_log, first_head, per_owner)
    gain_own = lax.dynamic_slice_in_dim(d_skip, first_head, per_owner)

    x4 = x_act.reshape(rows, owners, per_owner, head_width)
    g4 = grad_out.reshape(rows, owners, per_owner, head_width)
    r3 = dt_raw.reshape(rows, owners, per_owner)
    x_parts, raw_parts = [], []
    grad_b_all = None
    grad_c_all = None
    for c in range(chunks):
        sl = slice(c * per_chunk, (c + 1) * per_chunk)
        width = per_chunk * head_width
        x_in = x4[:, :, sl, :].reshape(rows, owners, width)
        g_in = g4[:, :, sl, :].reshape(rows, owners, width)
        if c == 0:
            g_in, _ = lax.optimization_barrier((g_in, own_seq))
        x_seq = lax.all_to_all(x_in, "ctx", split_axis=1, concat_axis=0, tiled=True).reshape(rows * owners, width)
        g_seq = lax.all_to_all(g_in, "ctx", split_axis=1, concat_axis=0, tiled=True).reshape(rows * owners, width)
        raw_seq = lax.all_to_all(r3[:, :, sl], "ctx", split_axis=1, concat_axis=0, tiled=True).reshape(
            rows * owners, per_chunk
        )
        x_back, raw_back, gb, gc = chunk_backward(
            x_seq, g_seq, raw_seq, b_rows, c_rows, rate_own[sl], gain_own[sl]
        )
        x_parts.append(
            lax.all_to_all(x_back, "ctx", split_axis=0, concat_axis=1, tiled=True).reshape(rows, owners, 1, width)
        )
        raw_parts.append(raw_back)
        grad_b_all = gb if grad_b_all is None else grad_b_all + gb
        grad_c_all = gc if grad_c_all is None else grad_c_all + gc
    grad_x = jnp.concatenate(x_parts, axis=2).reshape(rows, owners * per_owner * head_width)
    raw_all = jnp.concatenate(raw_parts, axis=1)

    is_first = half == 0
    send = jnp.where(is_first, grad_c_all, grad_b_all)
    keep = jnp.where(is_first, grad_b_all, grad_c_all)
    mine = keep + lax.ppermute(send, "tp", [(0, 1), (1, 0)])
    steps_back = raw_all.reshape(owners, rows, per_owner).transpose(0, 2, 1)
    extra = (per_owner * rows) // state
    if extra * state == per_owner * rows:
        packed = jnp.concatenate([mine.reshape(owners, rows, state), steps_back.reshape(owners, extra, state)], axis=1)
        parts = lax.all_to_all(packed, "ctx", split_axis=0, concat_axis=0, tiled=True)
        mine = parts[:, :rows, :].sum(axis=0)
        got_dt = parts[:, rows:, :].reshape(owners, per_owner, rows)
    else:
        parts = lax.all_to_all(mine.reshape(owners, rows, state), "ctx", split_axis=0, concat_axis=0, tiled=True)
        mine = parts.sum(axis=0)
        got_dt = lax.all_to_all(steps_back, "ctx", split_axis=0, concat_axis=0, tiled=True)
    grad_dt = got_dt.transpose(2, 0, 1).reshape(rows, heads_here).astype(jnp.bfloat16)
    other = lax.ppermute(mine, "tp", [(0, 1), (1, 0)])
    grad_b = jnp.where(is_first, mine, other)
    grad_c = jnp.where(is_first, other, mine)
    return (grad_x, grad_b, grad_c, grad_dt)


def solution(mesh):
    in_specs = (
        P("ctx", "tp"),
        P("ctx", None),
        P("ctx", None),
        P("ctx", "tp"),
        P("tp"),
        P("tp"),
        P("ctx", "tp"),
    )
    out_specs = (P("ctx", "tp"), P("ctx", None), P("ctx", None), P("ctx", "tp"))
    return jax.shard_map(local, mesh=mesh, in_specs=in_specs, out_specs=out_specs, check_vma=False)
```

```python
from functools import partial

import jax
import jax.numpy as jnp
from jax import lax
from jax.sharding import PartitionSpec as P

BLOCK = 256


precise = lax.Precision.HIGH


def head_forward(x_head, b_rows, c_rows, raw_step, log_rate, skip_gain, start_state, block_len):
    length, head_width = x_head.shape
    blocks = length // block_len
    step_size = jax.nn.softplus(raw_step)
    decay_rates = -jnp.exp(log_rate) * step_size
    row_index = lax.broadcasted_iota(jnp.int32, (block_len, block_len), 0)
    col_index = lax.broadcasted_iota(jnp.int32, (block_len, block_len), 1)
    lower_mask = row_index >= col_index
    running = jnp.dot(
        decay_rates.reshape(blocks, block_len), lower_mask.astype(jnp.float32).T, precision=precise
    )
    between = jnp.where(lower_mask[None], running[:, :, None] - running[:, None, :], -1e30)
    x_blocks = x_head.reshape(blocks, block_len, head_width)
    b_blocks = b_rows.reshape(blocks, block_len, -1)
    c_blocks = c_rows.reshape(blocks, block_len, -1)
    s_blocks = step_size.reshape(blocks, block_len)
    scores = (
        jnp.einsum("kin,kjn->kij", c_blocks, b_blocks, precision=precise)
        * jnp.exp(between)
        * s_blocks[:, None, :]
    )
    output = jnp.einsum("kij,kjp->kip", scores, x_blocks, precision=precise)
    closing = running[:, -1]
    weighted = (jnp.exp(closing[:, None] - running) * s_blocks)[:, :, None] * x_blocks
    states = jnp.einsum("kjp,kjn->kpn", weighted, b_blocks, precision=precise)
    block_rows = lax.broadcasted_iota(jnp.int32, (blocks, blocks), 0)
    block_cols = lax.broadcasted_iota(jnp.int32, (blocks, blocks), 1)
    through = jnp.dot((block_rows >= block_cols).astype(jnp.float32), closing, precision=precise)
    before = through - closing
    carry_weight = jnp.exp(
        jnp.where(block_rows > block_cols, before[:, None] - through[None, :], -1e30)
    )
    entering = (
        jnp.einsum("kj,jpn->kpn", carry_weight, states, precision=precise)
        + jnp.exp(before)[:, None, None] * start_state[None]
    )
    reading = jnp.exp(running)[:, :, None] * c_blocks
    output = output + jnp.einsum("kin,kpn->kip", reading, entering, precision=precise)
    output = output.reshape(length, head_width) + skip_gain * x_head
    final_state = (
        jnp.einsum("j,jpn->pn", jnp.exp(through[-1] - through), states, precision=precise)
        + jnp.exp(through[-1]) * start_state
    )
    return (output, final_state)


N_CHUNKS = 1


def chunk_backward(x_seq, g_seq, raw_seq, b_rows, c_rows, rate, gain):
    length = x_seq.shape[0]
    heads = raw_seq.shape[1]
    head_width = x_seq.shape[1] // heads
    runner = partial(head_forward, block_len=BLOCK)
    mapped = jax.vmap(runner, in_axes=(0, None, None, 0, 0, 0, 0))
    x_heads = x_seq.astype(jnp.float32).reshape(length, heads, head_width).transpose(1, 0, 2)
    g_heads = g_seq.astype(jnp.float32).reshape(length, heads, head_width).transpose(1, 0, 2)
    raw_heads = raw_seq.astype(jnp.float32).T
    anchor = jnp.zeros((heads, head_width, b_rows.shape[1]), jnp.float32)

    def forward(x_val, b_val, c_val, raw_val):
        return mapped(x_val, b_val, c_val, raw_val, rate, gain, anchor)[0]

    _, pullback = jax.vjp(forward, x_heads, b_rows, c_rows, raw_heads)
    grad_xh, grad_b_all, grad_c_all, grad_raw = pullback(g_heads)
    x_back = grad_xh.transpose(1, 0, 2).reshape(length, heads * head_width).astype(jnp.bfloat16)
    raw_back = grad_raw.T
    return x_back, raw_back, grad_b_all, grad_c_all


def gather_ctx(block, owners, me):
    if owners & (owners - 1):
        return lax.all_gather(block, "ctx", axis=0, tiled=True)
    have = block
    step = 1
    while step < owners:
        theirs = lax.ppermute(have, "ctx", [(k, k ^ step) for k in range(owners)])
        upper = (me // step) % 2 == 1
        have = jnp.where(upper, jnp.concatenate([theirs, have]), jnp.concatenate([have, theirs]))
        step *= 2
    return have


def local(x_act, b_proj, c_proj, dt_raw, a_log, d_skip, grad_out):
    rows = x_act.shape[0]
    heads_here = dt_raw.shape[1]
    head_width = x_act.shape[1] // heads_here
    state = b_proj.shape[1]
    owners = lax.axis_size("ctx")
    per_owner = heads_here // owners
    chunks = N_CHUNKS if per_owner % N_CHUNKS == 0 else 1
    per_chunk = per_owner // chunks
    me = lax.axis_index("ctx")
    half = lax.axis_index("tp")

    own_seq = gather_ctx(jnp.where(half == 0, b_proj, c_proj), owners, me)
    other_seq = lax.ppermute(own_seq, "tp", [(0, 1), (1, 0)])
    b_rows = jnp.where(half == 0, own_seq, other_seq).astype(jnp.float32)
    c_rows = jnp.where(half == 0, other_seq, own_seq).astype(jnp.float32)
    first_head = me * per_owner
    rate_own = lax.dynamic_slice_in_dim(a_log, first_head, per_owner)
    gain_own = lax.dynamic_slice_in_dim(d_skip, first_head, per_owner)

    x4 = x_act.reshape(rows, owners, per_owner, head_width)
    g4 = grad_out.reshape(rows, owners, per_owner, head_width)
    r3 = dt_raw.reshape(rows, owners, per_owner)
    x_parts, raw_parts = [], []
    grad_b_all = None
    grad_c_all = None
    for c in range(chunks):
        sl = slice(c * per_chunk, (c + 1) * per_chunk)
        width = per_chunk * head_width
        x_in = x4[:, :, sl, :].reshape(rows, owners, width)
        g_in = g4[:, :, sl, :].reshape(rows, owners, width)
        if c == 0:
            g_in, _ = lax.optimization_barrier((g_in, own_seq))
        x_seq = lax.all_to_all(x_in, "ctx", split_axis=1, concat_axis=0, tiled=True).reshape(rows * owners, width)
        g_seq = lax.all_to_all(g_in, "ctx", split_axis=1, concat_axis=0, tiled=True).reshape(rows * owners, width)
        raw_seq = lax.all_to_all(r3[:, :, sl], "ctx", split_axis=1, concat_axis=0, tiled=True).reshape(
            rows * owners, per_chunk
        )
        x_back, raw_back, gb, gc = chunk_backward(
            x_seq, g_seq, raw_seq, b_rows, c_rows, rate_own[sl], gain_own[sl]
        )
        x_parts.append(x_back)
        raw_parts.append(raw_back)
        grad_b_all = gb if grad_b_all is None else grad_b_all + gb
        grad_c_all = gc if grad_c_all is None else grad_c_all + gc
    raw_all = jnp.concatenate(raw_parts, axis=1)

    is_first = half == 0
    send = jnp.where(is_first, grad_c_all, grad_b_all)
    keep = jnp.where(is_first, grad_b_all, grad_c_all)
    mine = keep + lax.ppermute(send, "tp", [(0, 1), (1, 0)])
    steps_back = raw_all.reshape(owners, rows, per_owner).transpose(0, 2, 1)
    extra = (per_owner * rows) // state
    if extra * state == per_owner * rows:
        packed = jnp.concatenate([mine.reshape(owners, rows, state), steps_back.reshape(owners, extra, state)], axis=1)
        parts = lax.all_to_all(packed, "ctx", split_axis=0, concat_axis=0, tiled=True)
        mine = parts[:, :rows, :].sum(axis=0)
        got_dt = parts[:, rows:, :].reshape(owners, per_owner, rows)
    else:
        parts = lax.all_to_all(mine.reshape(owners, rows, state), "ctx", split_axis=0, concat_axis=0, tiled=True)
        mine = parts.sum(axis=0)
        got_dt = lax.all_to_all(steps_back, "ctx", split_axis=0, concat_axis=0, tiled=True)
    grad_dt = got_dt.transpose(2, 0, 1).reshape(rows, heads_here).astype(jnp.bfloat16)
    sent = []
    for part in x_parts:
        part, _ = lax.optimization_barrier((part, parts))
        sent.append(
            lax.all_to_all(part, "ctx", split_axis=0, concat_axis=1, tiled=True).reshape(rows, owners, 1, -1)
        )
    grad_x = jnp.concatenate(sent, axis=2).reshape(rows, owners * per_owner * head_width)
    other = lax.ppermute(mine, "tp", [(0, 1), (1, 0)])
    grad_b = jnp.where(is_first, mine, other)
    grad_c = jnp.where(is_first, other, mine)
    return (grad_x, grad_b, grad_c, grad_dt)


def solution(mesh):
    in_specs = (
        P("ctx", "tp"),
        P("ctx", None),
        P("ctx", None),
        P("ctx", "tp"),
        P("tp"),
        P("tp"),
        P("ctx", "tp"),
    )
    out_specs = (P("ctx", "tp"), P("ctx", None), P("ctx", None), P("ctx", "tp"))
    return jax.shard_map(local, mesh=mesh, in_specs=in_specs, out_specs=out_specs, check_vma=False)
```
